512 devices in a mesh: length: 16 (over z, core), girth: 32 (over x, y).
Axes of the slice: x: 4, y: 8, z: 8, core: 2. Of those that a mesh axis runs over, the one named last changes fastest.
Arguments:
- wave_amplitude: bfloat16 [6, 2048, 65536], P(None, 'length', 'girth'), may hold values from -6 to 6
- load_bank: bfloat16 [65536, 256], P('girth'), may hold values from -0.125 to 0.125
- freq_owner: int32 [1], replicated, may hold values from 0 to 31
- thickness_class: int32 [2048, 8192], P('length', 'girth'), may hold values from 0 to 7
- class_stiffness: float32 [8], replicated, may hold values from 0.5 to 4
- coupling: float32 [6, 6], replicated, may hold values from -0.15 to 2, as said below
- stress_map: float32 [4, 6], replicated, may hold values from -2.5 to 2.5
- psd_weight: float32 [1], replicated, may hold values from 0.5 to 2
- hotspot_tile: int32 [16, 1024], P('length', 'girth'), may hold values from 0 to 127
- hotspot_owner: int32 [16, 1024, 1], P('length', 'girth'), may hold values from 0 to 31; in each aligned block of 32 rows (0 to 31, 32 to 63, ..., all dimensions but the last counted through in order) at most 2 rows name the same one
- prior_moments: float32 [16, 32, 32, 2, 2, 256], P('length', 'girth'), may hold values from 0.1 to 1
Outputs:
- response: float32 [6, 2048, 8192], P(None, 'length', 'girth')
- hotspot_moments: float32 [16, 32, 32, 2, 2, 256], P('length', 'girth')
The draws below stay inside these ranges and needn't reach their ends.
Inputs may be any that keep to these rules, and one draw needn't show every extreme that they name: `hotspot_owner`: in each device's list of 32 hotspots no owner is named more than 2 times, and in some lists an owner is named exactly 2 times. `coupling`: Symmetric; each diagonal entry is at least 1 and exceeds the sum of the magnitudes of the other entries of its row.
All inputs are finite; a program needn't handle non-finite values.
Results may differ from the reference program's by a relative error of at most 0.0003.
Values may be sent and summed in bfloat16 or wider, within the bound.
No kernel may reach another device: no remote copies, remote signals or barrier semaphores. Data moves between devices by JAX's collectives and lax.ppermute only.
A program may use at most 64 MiB of HBM per device.

```python
import math
import jax
import jax.numpy as jnp
import numpy as np
from jax import lax

CL = 128
CG = 256
MODES = 2048
NCLASS = 8
SWEEPS = 4
CAP = 2
HS_DEV = 32
NLEN = 2048
NGIR = 8192
N_LENGTH = 16
N_GIRTH = 32


def draw_coupling(key, part):
    first, second = jax.random.split(jax.random.fold_in(key, 17))
    diag_part = jax.random.uniform(first, (6,), jnp.float32, 1.0, 2.0)
    raw = jax.random.uniform(second, (6, 6), jnp.float32, -0.15, 0.15)
    eye_mask = jnp.eye(6, dtype=jnp.float32)
    off_part = 0.5 * (raw + raw.T) * (1.0 - eye_mask)
    return off_part + eye_mask * diag_part[None, :]


def set_ends(values, stream_key, smallest, high):
    longest = values.shape.index(max(values.shape))
    spots = []
    for shift in (0, 1):
        where = [jax.random.randint(jax.random.fold_in(stream_key, axis), (), 0, length) for axis, length in enumerate(values.shape)]
        where[longest] = (where[longest] + shift) % values.shape[longest]
        spots.append(tuple(where))
    return values.at[spots[0]].set(smallest).at[spots[1]].set(high)


def steps_of(stream_key, shape, cuts, smallest, largest):
    loudness, own = 1.0, jax.random.fold_in(stream_key, 6)
    for dim, parts in cuts:
        draws = jnp.exp(jax.random.uniform(jax.random.fold_in(own, dim), (parts,), jnp.float32, smallest / len(cuts), largest / len(cuts)))
        loudness = loudness * jnp.repeat(draws, shape[dim] // parts).reshape([-1 if axis == dim else 1 for axis in range(len(shape))])
    return loudness


def deal_out(own_key, own, number, rows, count, top, reach, slope):
    sequence = jax.random.permutation(own_key, count)
    heavy_load, usual = portions_of(count, rows * top, reach, slope, True), portions_of(count, rows * top, reach, slope, False)
    places = jnp.arange(count)

    def named(tallies, turn):
        used = int((tallies > 0).sum())
        fixed = max(1, used // 4)
        moved = fixed + (places - fixed + turn * (used - fixed)) % max(1, count - fixed)
        return jnp.zeros((count,), jnp.int32).at[sequence[jnp.where(places < fixed, places, moved)]].set(jnp.asarray(tallies, jnp.int32))

    tallies = jnp.where(number % 4 == 0, named(heavy_load, number // 4), named(usual, number - number // 4 - 1))
    mixed = jax.random.permutation(jax.random.fold_in(own, 3), count)
    donor, receiver = mixed[0:count // 2 * 2:2], mixed[1:count // 2 * 2:2]
    slack = jnp.minimum(tallies[donor] - 1, reach - tallies[receiver]) // 2
    slack = jnp.where((donor == sequence[0]) | (receiver == sequence[0]) | (tallies[receiver] == 0), 0, jnp.maximum(slack, 0))
    moved = jax.random.randint(jax.random.fold_in(own, 4), (count // 2,), 0, 1 << 20) % (slack + 1)
    tallies = tallies.at[donor].add(-moved).at[receiver].add(moved)
    labels = jnp.searchsorted(jnp.cumsum(tallies), jnp.arange(rows * top), side="right").astype(jnp.int32)
    grid = labels.reshape(top, rows).T
    grid = grid[jax.random.permutation(jax.random.fold_in(own, 1), rows)]
    turn = jax.random.randint(jax.random.fold_in(own, 2), (rows, 1), 0, top)
    return jnp.take_along_axis(grid, (jnp.arange(top)[None, :] + turn) % top, axis=1)


def portions_of(amount, total, bound, slope, full):
    portions = [(1 << 20) // math.isqrt(grade ** slope) + 1 for grade in range(1, amount + 1)]
    largest = bound if full else min(bound, max(-(-total // amount), total * portions[0] // sum(portions)))
    least = 1 if total - largest >= amount - 1 else 0
    holding, rest = [largest] + [least] * (amount - 1), total - largest - least * (amount - 1)
    while rest > 0:
        candidates = [i for i in range(1, amount) if holding[i] < largest] or [i for i in range(1, amount) if holding[i] < bound]
        mass, budget = sum([portions[i] for i in candidates]), rest
        for i in candidates:
            more = min(bound - holding[i], max(1, budget * portions[i] // mass), rest)
            holding[i] = holding[i] + more
            rest = rest - more
    return np.array(holding)


def noise(key, shape, scale, bound, cuts=(), kind=jnp.bfloat16):
    factor_of = steps_of(key, shape, cuts, -0.22, 0.18) if cuts else 1.0
    array = jax.random.normal(key, shape, jnp.float32) * scale * factor_of
    return jnp.minimum(jnp.maximum(array, -bound), bound).astype(kind)


def setup_inputs(seed: int = 0) -> dict:
    arg_keys = jax.random.split(jax.random.key(seed), 12)
    wave_amplitude = noise(arg_keys[0], (6, NLEN, N_GIRTH * MODES), 1.0, 6.0, ((1, 16), (2, 32)))
    load_bank = noise(arg_keys[1], (N_GIRTH * MODES, CG), MODES ** -0.5, 0.125, ((0, 32),))
    freq_owner = jax.random.randint(arg_keys[2], (1,), 0, N_GIRTH).astype(jnp.int32)
    thickness_class = set_ends(jax.random.randint(arg_keys[3], (NLEN, NGIR), 0, NCLASS), jax.random.fold_in(arg_keys[3], 1), 0, NCLASS - 1).astype(jnp.int32)
    class_stiffness = jnp.clip(jnp.exp(jax.random.uniform(arg_keys[4], (NCLASS,), jnp.float32, math.log(0.5), math.log(4.0))), 0.5, 4.0)
    coupling = draw_coupling(jax.random.fold_in(arg_keys[11], 71), 0)
    stress_map = noise(arg_keys[6], (4, 6), 6 ** -0.5, 2.5, (), jnp.float32)
    psd_weight = jnp.clip(jnp.exp(jax.random.uniform(arg_keys[7], (1,), jnp.float32, math.log(0.5), math.log(2.0))), 0.5, 2.0)
    hotspot_tile = set_ends(jax.random.randint(arg_keys[8], (N_LENGTH, N_GIRTH * HS_DEV), 0, CL), jax.random.fold_in(arg_keys[8], 1), 0, CL - 1).astype(jnp.int32)
    hotspot_owner_keys = jax.random.split(jax.random.fold_in(arg_keys[9], 1), N_LENGTH * (N_GIRTH * HS_DEV) // HS_DEV)
    hotspot_owner_turns = jax.random.permutation(jax.random.fold_in(arg_keys[9], 3), N_LENGTH * (N_GIRTH * HS_DEV) // HS_DEV)
    hotspot_owner = jax.vmap(lambda own, number: deal_out(jax.random.fold_in(arg_keys[9], 2), own, number, HS_DEV, N_GIRTH, 1, CAP, 2))(hotspot_owner_keys, hotspot_owner_turns).reshape((N_LENGTH, N_GIRTH * HS_DEV, 1))
    prior_moments = jnp.clip(jnp.exp(math.log(1.0) - 2.3025851 * jax.random.uniform(arg_keys[10], (N_LENGTH, N_GIRTH, N_GIRTH, CAP, 2, CG), jnp.float32) ** steps_of(arg_keys[10], (N_LENGTH, N_GIRTH, N_GIRTH, CAP, 2, CG), ((0, 16), (1, 32)), -0.2, 0.2)), 0.1, 1.0)
    return {"wave_amplitude": wave_amplitude, "load_bank": load_bank, "freq_owner": freq_owner, "thickness_class": thickness_class, "class_stiffness": class_stiffness, "coupling": coupling, "stress_map": stress_map, "psd_weight": psd_weight, "hotspot_tile": hotspot_tile, "hotspot_owner": hotspot_owner, "prior_moments": prior_moments}


def chebyshev_weight(sweep):
    return 1.0 / (1.0 + 0.9 * math.cos(math.pi * (2 * sweep + 1) / (2 * SWEEPS)))


def operate_padded(padded, stiffness, coupling):
    centre = padded[:, 1:-1, 1:-1]
    beside = padded[:, 2:, 1:-1] + padded[:, :-2, 1:-1] + padded[:, 1:-1, 2:] + padded[:, 1:-1, :-2]
    mixing = jnp.einsum('ab,bij->aij', coupling, centre, precision=lax.Precision.HIGHEST)
    return stiffness * (4.0 * centre - beside) + mixing


def reference(wave_amplitude, load_bank, freq_owner, thickness_class, class_stiffness, coupling, stress_map, psd_weight, hotspot_tile, hotspot_owner, prior_moments):
    owner = freq_owner[0].astype(jnp.int32)
    factors = lax.dynamic_slice_in_dim(load_bank, owner * MODES, MODES, 0)

    def tile_loading(tile_index):
        amplitude = lax.dynamic_slice_in_dim(wave_amplitude, tile_index * MODES, MODES, 2)
        amplitude = amplitude.reshape(6 * NLEN, MODES)
        return jnp.dot(amplitude, factors, preferred_element_type=jnp.float32).reshape(6, NLEN, CG)

    pieces = lax.map(tile_loading, jnp.arange(N_GIRTH, dtype=jnp.int32))
    loading = jnp.transpose(pieces, (1, 2, 0, 3)).reshape(6, NLEN, NGIR)
    stiffness = class_stiffness[thickness_class]
    diagonal = 4.0 * stiffness[None] + jnp.diagonal(coupling)[:, None, None]
    motion = jnp.zeros((6, NLEN, NGIR), jnp.float32)
    for sweep in range(SWEEPS):
        padded = jnp.pad(motion, ((0, 0), (1, 1), (1, 1)))
        applied = operate_padded(padded, stiffness, coupling)
        motion = motion + chebyshev_weight(sweep) * ((loading - applied) / diagonal)
    stresses = stiffness[None] * jnp.einsum('ka,aij->kij', stress_map, motion, precision=lax.Precision.HIGHEST)
    stress_five = stresses.reshape(4, N_LENGTH, CL, N_GIRTH, CG)
    tile_ids = hotspot_tile.reshape(N_LENGTH, N_GIRTH, HS_DEV).astype(jnp.int32)
    owner_ids = hotspot_owner.reshape(N_LENGTH, N_GIRTH, HS_DEV).astype(jnp.int32)
    length_ids = jnp.arange(N_LENGTH, dtype=jnp.int32)[:, None, None]
    girth_ids = jnp.arange(N_GIRTH, dtype=jnp.int32)[None, :, None]
    picked = stress_five[:, length_ids, tile_ids, girth_ids, :]
    picked = jnp.moveaxis(picked, 0, 3)
    spectra = jnp.stack([picked[..., 0, :] * picked[..., 0, :] + picked[..., 1, :] * picked[..., 1, :],
                         picked[..., 2, :] * picked[..., 2, :] + picked[..., 3, :] * picked[..., 3, :]], axis=3)
    positions = jnp.arange(HS_DEV, dtype=jnp.int32)
    matching = owner_ids[..., :, None] == owner_ids[..., None, :]
    earlier = positions[None, :] < positions[:, None]
    slot_rank = jnp.sum(jnp.logical_and(matching, earlier).astype(jnp.int32), axis=-1).astype(jnp.int32)
    increment = jnp.zeros((N_LENGTH, N_GIRTH, N_GIRTH, CAP, 2, CG), jnp.float32)
    increment = increment.at[length_ids, owner_ids, girth_ids, slot_rank].set(spectra)
    hotspot_moments = prior_moments + psd_weight[0] * increment
    return motion, hotspot_moments
```

```python
import math

import jax
import jax.numpy as jnp
from jax import lax
from jax.sharding import PartitionSpec as P

SWEEPS = 4
CAP = 2


def scatter_gather(block, axis, source):
    count = lax.axis_size(axis)
    rows = block.shape[0]
    send = block.reshape(count, rows // count, block.shape[1])
    got = lax.all_to_all(send, axis, 0, 0, tiled=True)
    mine = lax.dynamic_index_in_dim(got, source, 0, keepdims=False)
    send = jnp.broadcast_to(mine[None], (count,) + mine.shape)
    full = lax.all_to_all(send, axis, 0, 0, tiled=True)
    return full.reshape(rows, block.shape[1])


def spread(block, axis, source, pair_axis):
    core = lax.axis_index(pair_axis) % 2
    half = block.shape[0] // 2
    mine = lax.dynamic_slice_in_dim(block, core * half, half, 0)
    got = scatter_gather(mine, axis, source)
    pairs = [(i, i ^ 1) for i in range(lax.axis_size(pair_axis))]
    other = lax.ppermute(got, pair_axis, pairs)
    low = jnp.where(core == 0, got, other)
    high = jnp.where(core == 0, other, got)
    return jnp.concatenate([low, high], axis=0)


def padded_2(block, sides, width):
    for axis, dim in sides:
        count = lax.axis_size(axis)
        forward = [(i, i + 1) for i in range(count - 1)]
        backward = [(target, source) for source, target in forward]
        low = lax.ppermute(
            lax.slice_in_dim(block, block.shape[dim] - width, None, axis=dim), axis, forward
        )
        high = lax.ppermute(lax.slice_in_dim(block, 0, width, axis=dim), axis, backward)
        block = jnp.concatenate([low, block, high], axis=dim)
    return block


def chebyshev_weight(sweep):
    return 1.0 / (1.0 + 0.9 * math.cos(math.pi * (2 * sweep + 1) / (2 * SWEEPS)))


def operate_padded(padded, stiffness, coupling):
    centre = padded[:, 1:-1, 1:-1]
    beside = padded[:, 2:, 1:-1] + padded[:, :-2, 1:-1] + padded[:, 1:-1, 2:] + padded[:, 1:-1, :-2]
    mixing = jnp.einsum("ab,bij->aij", coupling, centre, precision=lax.Precision.HIGHEST)
    return stiffness * (4.0 * centre - beside) + mixing


def square_pairs(values, axis_at):
    first = jnp.take(values, 0, axis=axis_at)
    second = jnp.take(values, 1, axis=axis_at)
    third = jnp.take(values, 2, axis=axis_at)
    fourth = jnp.take(values, 3, axis=axis_at)
    return jnp.stack(
        [first * first + second * second, third * third + fourth * fourth], axis=axis_at
    )


def on_device(
    wave_amplitude,
    load_bank,
    freq_owner,
    thickness_class,
    class_stiffness,
    coupling,
    stress_map,
    psd_weight,
    hotspot_tile,
    hotspot_owner,
    prior_moments,
):
    row_count = wave_amplitude.shape[1]
    girth_cells = load_bank.shape[1]
    mode_count = load_bank.shape[0]
    amplitude = wave_amplitude.reshape(6 * row_count, mode_count)
    root = freq_owner[0]
    factors = spread(load_bank, "girth", root, "length")
    loading = jnp.dot(amplitude, factors, preferred_element_type=jnp.float32)
    loading = loading.reshape(6, row_count, girth_cells)
    stiffness = jnp.zeros((row_count, girth_cells), jnp.float32)
    for level in range(class_stiffness.shape[0]):
        stiffness = stiffness + jnp.where(thickness_class == level, class_stiffness[level], 0.0)
    coupling_diag = jnp.diagonal(coupling)[:, None, None]
    diagonal = 4.0 * stiffness[None] + coupling_diag
    motion = chebyshev_weight(0) * (loading / diagonal)
    for sweep in range(1, SWEEPS):
        padded = padded_2(motion, (("length", 1), ("girth", 2)), 1)
        applied = operate_padded(padded, stiffness, coupling)
        motion = motion + chebyshev_weight(sweep) * ((loading - applied) / diagonal)
    girth_count = lax.axis_size("girth")
    tile_ids = hotspot_tile[0]
    owner_ids = hotspot_owner[0, :, 0]
    listed = owner_ids.shape[0]
    positions = jnp.arange(listed, dtype=jnp.int32)
    matching = owner_ids[:, None] == owner_ids[None, :]
    earlier = positions[None, :] < positions[:, None]
    slot_rank = jnp.sum(jnp.logical_and(matching, earlier).astype(jnp.int32), axis=1)
    target = owner_ids * CAP + slot_rank
    stresses = stiffness[:, None, :] * jnp.einsum(
        "ka,aij->ikj", stress_map, motion, precision=lax.Precision.HIGHEST
    )
    stress_rows = jnp.take(stresses, tile_ids, axis=0)
    outbox = jnp.zeros((girth_count * CAP, 4, girth_cells), jnp.float32).at[target].set(stress_rows)
    outbox = outbox.reshape(girth_count, CAP, 4, girth_cells)
    received = lax.all_to_all(outbox, "girth", split_axis=0, concat_axis=0, tiled=True)
    hotspot_moments = prior_moments + (psd_weight[0] * square_pairs(received, 2))[None, None]
    return (motion, hotspot_moments)


def solution(mesh):
    return jax.shard_map(
        on_device,
        mesh=mesh,
        in_specs=(
            P(None, "length", "girth"),
            P("girth", None),
            P(),
            P("length", "girth"),
            P(),
            P(),
            P(),
            P(),
            P("length", "girth"),
            P("length", "girth", None),
            P("length", "girth", None, None, None, None),
        ),
        out_specs=(P(None, "length", "girth"), P("length", "girth", None, None, None, None)),
        check_vma=False,
    )
```

```python
import math

import jax
import jax.numpy as jnp
from jax import lax
from jax.sharding import PartitionSpec as P

SWEEPS = 4
CAP = 2


def scatter_gather(block, axis, source):
    count = lax.axis_size(axis)
    rows = block.shape[0]
    send = block.reshape(count, rows // count, block.shape[1])
    got = lax.all_to_all(send, axis, 0, 0, tiled=True)
    mine = lax.dynamic_index_in_dim(got, source, 0, keepdims=False)
    send = jnp.broadcast_to(mine[None], (count,) + mine.shape)
    full = lax.all_to_all(send, axis, 0, 0, tiled=True)
    return full.reshape(rows, block.shape[1])


def spread(block, axis, source, pair_axis):
    core = lax.axis_index(pair_axis) % 2
    half = block.shape[0] // 2
    mine = lax.dynamic_slice_in_dim(block, core * half, half, 0)
    got = scatter_gather(mine, axis, source)
    pairs = [(i, i ^ 1) for i in range(lax.axis_size(pair_axis))]
    other = lax.ppermute(got, pair_axis, pairs)
    low = jnp.where(core == 0, got, other)
    high = jnp.where(core == 0, other, got)
    return jnp.concatenate([low, high], axis=0)


def padded_2(block, sides, width):
    for axis, dim in sides:
        count = lax.axis_size(axis)
        forward = [(i, i + 1) for i in range(count - 1)]
        backward = [(target, source) for source, target in forward]
        low = lax.ppermute(
            lax.slice_in_dim(block, block.shape[dim] - width, None, axis=dim), axis, forward
        )
        high = lax.ppermute(lax.slice_in_dim(block, 0, width, axis=dim), axis, backward)
        block = jnp.concatenate([low, block, high], axis=dim)
    return block


def chebyshev_weight(sweep):
    return 1.0 / (1.0 + 0.9 * math.cos(math.pi * (2 * sweep + 1) / (2 * SWEEPS)))


def operate_padded(padded, stiffness, coupling):
    centre = padded[:, 1:-1, 1:-1]
    beside = padded[:, 2:, 1:-1] + padded[:, :-2, 1:-1] + padded[:, 1:-1, 2:] + padded[:, 1:-1, :-2]
    mixing = jnp.einsum("ab,bij->aij", coupling, centre, precision=lax.Precision.HIGHEST)
    return stiffness * (4.0 * centre - beside) + mixing


def square_pairs(values, axis_at):
    first = jnp.take(values, 0, axis=axis_at)
    second = jnp.take(values, 1, axis=axis_at)
    third = jnp.take(values, 2, axis=axis_at)
    fourth = jnp.take(values, 3, axis=axis_at)
    return jnp.stack(
        [first * first + second * second, third * third + fourth * fourth], axis=axis_at
    )


def on_device(
    wave_amplitude,
    load_bank,
    freq_owner,
    thickness_class,
    class_stiffness,
    coupling,
    stress_map,
    psd_weight,
    hotspot_tile,
    hotspot_owner,
    prior_moments,
):
    row_count = wave_amplitude.shape[1]
    girth_cells = load_bank.shape[1]
    mode_count = load_bank.shape[0]
    amplitude = wave_amplitude.reshape(6 * row_count, mode_count)
    root = freq_owner[0]
    factors = spread(load_bank, "girth", root, "length")
    loading = jnp.dot(amplitude, factors, preferred_element_type=jnp.float32)
    loading = loading.reshape(6, row_count, girth_cells)
    stiffness = jnp.zeros((row_count, girth_cells), jnp.float32)
    for level in range(class_stiffness.shape[0]):
        stiffness = stiffness + jnp.where(thickness_class == level, class_stiffness[level], 0.0)
    coupling_diag = jnp.diagonal(coupling)[:, None, None]
    width = SWEEPS - 1
    packed = jnp.concatenate([loading, stiffness[None]], axis=0)
    packed = padded_2(packed, (("length", 1), ("girth", 2)), width)
    loading_ext = packed[:6]
    stiffness_ext = packed[6]
    diagonal_ext = 4.0 * stiffness_ext[None] + coupling_diag
    motion = chebyshev_weight(0) * (loading_ext / diagonal_ext)
    for sweep in range(1, SWEEPS):
        applied = operate_padded(motion, stiffness_ext[1:-1, 1:-1], coupling)
        loading_ext = loading_ext[:, 1:-1, 1:-1]
        stiffness_ext = stiffness_ext[1:-1, 1:-1]
        diagonal_ext = diagonal_ext[:, 1:-1, 1:-1]
        motion = motion[:, 1:-1, 1:-1] + chebyshev_weight(sweep) * ((loading_ext - applied) / diagonal_ext)
    girth_count = lax.axis_size("girth")
    tile_ids = hotspot_tile[0]
    owner_ids = hotspot_owner[0, :, 0]
    listed = owner_ids.shape[0]
    positions = jnp.arange(listed, dtype=jnp.int32)
    matching = owner_ids[:, None] == owner_ids[None, :]
    earlier = positions[None, :] < positions[:, None]
    slot_rank = jnp.sum(jnp.logical_and(matching, earlier).astype(jnp.int32), axis=1)
    target = owner_ids * CAP + slot_rank
    stiffness_rows = jnp.take(stiffness, tile_ids, axis=0)
    motion_rows = jnp.take(motion, tile_ids, axis=1)
    stress_rows = stiffness_rows[:, None, :] * jnp.einsum(
        "ka,aij->ikj", stress_map, motion_rows, precision=lax.Precision.HIGHEST
    )
    spectra = square_pairs(stress_rows, 1)
    outbox = jnp.zeros((girth_count * CAP, 2, girth_cells), jnp.float32).at[target].set(spectra)
    outbox = outbox.reshape(girth_count, CAP, 2, girth_cells)
    received = lax.all_to_all(outbox, "girth", split_axis=0, concat_axis=0, tiled=True)
    hotspot_moments = prior_moments + (psd_weight[0] * received)[None, None]
    return (motion, hotspot_moments)


def solution(mesh):
    return jax.shard_map(
        on_device,
        mesh=mesh,
        in_specs=(
            P(None, "length", "girth"),
            P("girth", None),
            P(),
            P("length", "girth"),
            P(),
            P(),
            P(),
            P(),
            P("length", "girth"),
            P("length", "girth", None),
            P("length", "girth", None, None, None, None),
        ),
        out_specs=(P(None, "length", "girth"), P("length", "girth", None, None, None, None)),
        check_vma=False,
    )
```

```python
import math

import jax
import jax.numpy as jnp
from jax import lax
from jax.sharding import PartitionSpec as P

SWEEPS = 4
CAP = 2


def scatter_gather(block, axis, source):
    count = lax.axis_size(axis)
    rows = block.shape[0]
    send = block.reshape(count, rows // count, block.shape[1])
    got = lax.all_to_all(send, axis, 0, 0, tiled=True)
    mine = lax.dynamic_index_in_dim(got, source, 0, keepdims=False)
    send = jnp.broadcast_to(mine[None], (count,) + mine.shape)
    full = lax.all_to_all(send, axis, 0, 0, tiled=True)
    return full.reshape(rows, block.shape[1])


def spread(block, axis, source, pair_axis):
    core = lax.axis_index(pair_axis) % 2
    half = block.shape[0] // 2
    mine = lax.dynamic_slice_in_dim(block, core * half, half, 0)
    got = scatter_gather(mine, axis, source)
    pairs = [(i, i ^ 1) for i in range(lax.axis_size(pair_axis))]
    other = lax.ppermute(got, pair_axis, pairs)
    low = jnp.where(core == 0, got, other)
    high = jnp.where(core == 0, other, got)
    return jnp.concatenate([low, high], axis=0)


def padded_2(block, sides, width):
    for axis, dim in sides:
        count = lax.axis_size(axis)
        forward = [(i, i + 1) for i in range(count - 1)]
        backward = [(target, source) for source, target in forward]
        low = lax.ppermute(
            lax.slice_in_dim(block, block.shape[dim] - width, None, axis=dim), axis, forward
        )
        high = lax.ppermute(lax.slice_in_dim(block, 0, width, axis=dim), axis, backward)
        block = jnp.concatenate([low, block, high], axis=dim)
    return block


def chebyshev_weight(sweep):
    return 1.0 / (1.0 + 0.9 * math.cos(math.pi * (2 * sweep + 1) / (2 * SWEEPS)))


def operate_padded(padded, stiffness, coupling):
    centre = padded[:, 1:-1, 1:-1]
    beside = padded[:, 2:, 1:-1] + padded[:, :-2, 1:-1] + padded[:, 1:-1, 2:] + padded[:, 1:-1, :-2]
    mixing = jnp.einsum("ab,bij->aij", coupling, centre, precision=lax.Precision.HIGHEST)
    return stiffness * (4.0 * centre - beside) + mixing


def square_pairs(values, axis_at):
    first = jnp.take(values, 0, axis=axis_at)
    second = jnp.take(values, 1, axis=axis_at)
    third = jnp.take(values, 2, axis=axis_at)
    fourth = jnp.take(values, 3, axis=axis_at)
    return jnp.stack(
        [first * first + second * second, third * third + fourth * fourth], axis=axis_at
    )


def on_device(
    wave_amplitude,
    load_bank,
    freq_owner,
    thickness_class,
    class_stiffness,
    coupling,
    stress_map,
    psd_weight,
    hotspot_tile,
    hotspot_owner,
    prior_moments,
):
    row_count = wave_amplitude.shape[1]
    girth_cells = load_bank.shape[1]
    mode_count = load_bank.shape[0]
    width = SWEEPS - 1
    root = freq_owner[0]
    stiffness = jnp.zeros((row_count, girth_cells), jnp.float32)
    for level in range(class_stiffness.shape[0]):
        stiffness = stiffness + jnp.where(thickness_class == level, class_stiffness[level], 0.0)
    amplitude_ext = padded_2(wave_amplitude, (("length", 1),), width)
    stiffness_rows = padded_2(stiffness, (("length", 0),), width)
    factors = spread(load_bank, "girth", root, "length")
    ext_rows = row_count + 2 * width
    loading = jnp.dot(amplitude_ext.reshape(6 * ext_rows, mode_count), factors, preferred_element_type=jnp.float32)
    loading = loading.reshape(6, ext_rows, girth_cells)
    coupling_diag = jnp.diagonal(coupling)[:, None, None]
    packed = jnp.concatenate([loading, stiffness_rows[None]], axis=0)
    packed = padded_2(packed, (("girth", 2),), width)
    loading_ext = packed[:6]
    stiffness_ext = packed[6]
    diagonal_ext = 4.0 * stiffness_ext[None] + coupling_diag
    motion = chebyshev_weight(0) * (loading_ext / diagonal_ext)
    for sweep in range(1, SWEEPS):
        applied = operate_padded(motion, stiffness_ext[1:-1, 1:-1], coupling)
        loading_ext = loading_ext[:, 1:-1, 1:-1]
        stiffness_ext = stiffness_ext[1:-1, 1:-1]
        diagonal_ext = diagonal_ext[:, 1:-1, 1:-1]
        motion = motion[:, 1:-1, 1:-1] + chebyshev_weight(sweep) * ((loading_ext - applied) / diagonal_ext)
    girth_count = lax.axis_size("girth")
    tile_ids = hotspot_tile[0]
    owner_ids = hotspot_owner[0, :, 0]
    listed = owner_ids.shape[0]
    positions = jnp.arange(listed, dtype=jnp.int32)
    matching = owner_ids[:, None] == owner_ids[None, :]
    earlier = positions[None, :] < positions[:, None]
    slot_rank = jnp.sum(jnp.logical_and(matching, earlier).astype(jnp.int32), axis=1)
    target = owner_ids * CAP + slot_rank
    slots = jnp.arange(girth_count * CAP, dtype=jnp.int32)
    hit = target[None, :] == slots[:, None]
    filled = jnp.any(hit, axis=1)
    slot_row = jnp.sum(jnp.where(hit, tile_ids[None, :], 0), axis=1)
    stiffness_at = jnp.take(stiffness, slot_row, axis=0)
    motion_at = jnp.take(motion, slot_row, axis=1)
    stress_rows = stiffness_at[:, None, :] * jnp.einsum(
        "ka,aij->ikj", stress_map, motion_at, precision=lax.Precision.HIGHEST
    )
    spectra = square_pairs(stress_rows, 1)
    outbox = jnp.where(filled[:, None, None], spectra, 0.0)
    outbox = outbox.reshape(girth_count, CAP, 2, girth_cells)
    received = lax.all_to_all(outbox, "girth", split_axis=0, concat_axis=0, tiled=True)
    hotspot_moments = prior_moments + (psd_weight[0] * received)[None, None]
    return (motion, hotspot_moments)


def solution(mesh):
    return jax.shard_map(
        on_device,
        mesh=mesh,
        in_specs=(
            P(None, "length", "girth"),
            P("girth", None),
            P(),
            P("length", "girth"),
            P(),
            P(),
            P(),
            P(),
            P("length", "girth"),
            P("length", "girth", None),
            P("length", "girth", None, None, None, None),
        ),
        out_specs=(P(None, "length", "girth"), P("length", "girth", None, None, None, None)),
        check_vma=False,
    )
```

```python
import math

import jax
import jax.numpy as jnp
from jax import lax
from jax.sharding import PartitionSpec as P

SWEEPS = 4
CAP = 2


def scatter_gather(block, axis, source):
    count = lax.axis_size(axis)
    rows = block.shape[0]
    send = block.reshape(count, rows // count, block.shape[1])
    got = lax.all_to_all(send, axis, 0, 0, tiled=True)
    mine = lax.dynamic_index_in_dim(got, source, 0, keepdims=False)
    send = jnp.broadcast_to(mine[None], (count,) + mine.shape)
    full = lax.all_to_all(send, axis, 0, 0, tiled=True)
    return full.reshape(rows, block.shape[1])


def spread(block, axis, source, pair_axis):
    core = lax.axis_index(pair_axis) % 2
    half = block.shape[0] // 2
    mine = lax.dynamic_slice_in_dim(block, core * half, half, 0)
    got = scatter_gather(mine, axis, source)
    pairs = [(i, i ^ 1) for i in range(lax.axis_size(pair_axis))]
    other = lax.ppermute(got, pair_axis, pairs)
    low = jnp.where(core == 0, got, other)
    high = jnp.where(core == 0, other, got)
    return jnp.concatenate([low, high], axis=0)


def padded_2(block, sides, width):
    for axis, dim in sides:
        count = lax.axis_size(axis)
        forward = [(i, i + 1) for i in range(count - 1)]
        backward = [(target, source) for source, target in forward]
        low = lax.ppermute(
            lax.slice_in_dim(block, block.shape[dim] - width, None, axis=dim), axis, forward
        )
        high = lax.ppermute(lax.slice_in_dim(block, 0, width, axis=dim), axis, backward)
        block = jnp.concatenate([low, block, high], axis=dim)
    return block


def padded_last(block, axis, width):
    count = lax.axis_size(axis)
    forward = [(i, i + 1) for i in range(count - 1)]
    backward = [(target, source) for source, target in forward]
    lead, rows = block.shape[0], block.shape[1]

    def pack(strip):
        return jnp.swapaxes(strip, 1, 2).reshape(lead * width, rows)

    def unpack(flat):
        return jnp.swapaxes(flat.reshape(lead, width, rows), 1, 2)

    low = unpack(lax.ppermute(pack(block[:, :, block.shape[2] - width :]), axis, forward))
    high = unpack(lax.ppermute(pack(block[:, :, :width]), axis, backward))
    return jnp.concatenate([low, block, high], axis=2)


def chebyshev_weight(sweep):
    return 1.0 / (1.0 + 0.9 * math.cos(math.pi * (2 * sweep + 1) / (2 * SWEEPS)))


def operate_padded(padded, stiffness, coupling):
    centre = padded[:, 1:-1, 1:-1]
    beside = padded[:, 2:, 1:-1] + padded[:, :-2, 1:-1] + padded[:, 1:-1, 2:] + padded[:, 1:-1, :-2]
    mixing = jnp.einsum("ab,bij->aij", coupling, centre, precision=lax.Precision.HIGHEST)
    return stiffness * (4.0 * centre - beside) + mixing


def square_pairs(values, axis_at):
    first = jnp.take(values, 0, axis=axis_at)
    second = jnp.take(values, 1, axis=axis_at)
    third = jnp.take(values, 2, axis=axis_at)
    fourth = jnp.take(values, 3, axis=axis_at)
    return jnp.stack(
        [first * first + second * second, third * third + fourth * fourth], axis=axis_at
    )


def on_device(
    wave_amplitude,
    load_bank,
    freq_owner,
    thickness_class,
    class_stiffness,
    coupling,
    stress_map,
    psd_weight,
    hotspot_tile,
    hotspot_owner,
    prior_moments,
):
    row_count = wave_amplitude.shape[1]
    girth_cells = load_bank.shape[1]
    mode_count = load_bank.shape[0]
    width = SWEEPS - 1
    root = freq_owner[0]
    stiffness = jnp.zeros((row_count, girth_cells), jnp.float32)
    for level in range(class_stiffness.shape[0]):
        stiffness = stiffness + jnp.where(thickness_class == level, class_stiffness[level], 0.0)
    amplitude_ext = padded_2(wave_amplitude, (("length", 1),), width)
    stiffness_rows = padded_2(stiffness, (("length", 0),), width)
    factors = spread(load_bank, "girth", root, "length")
    ext_rows = row_count + 2 * width
    loading = jnp.dot(amplitude_ext.reshape(6 * ext_rows, mode_count), factors, preferred_element_type=jnp.float32)
    loading = loading.reshape(6, ext_rows, girth_cells)
    coupling_diag = jnp.diagonal(coupling)[:, None, None]
    packed = jnp.concatenate([loading, stiffness_rows[None]], axis=0)
    packed = padded_last(packed, "girth", width)
    loading_ext = packed[:6]
    stiffness_ext = packed[6]
    diagonal_ext = 4.0 * stiffness_ext[None] + coupling_diag
    motion = chebyshev_weight(0) * (loading_ext / diagonal_ext)
    for sweep in range(1, SWEEPS):
        applied = operate_padded(motion, stiffness_ext[1:-1, 1:-1], coupling)
        loading_ext = loading_ext[:, 1:-1, 1:-1]
        stiffness_ext = stiffness_ext[1:-1, 1:-1]
        diagonal_ext = diagonal_ext[:, 1:-1, 1:-1]
        motion = motion[:, 1:-1, 1:-1] + chebyshev_weight(sweep) * ((loading_ext - applied) / diagonal_ext)
    girth_count = lax.axis_size("girth")
    tile_ids = hotspot_tile[0]
    owner_ids = hotspot_owner[0, :, 0]
    listed = owner_ids.shape[0]
    positions = jnp.arange(listed, dtype=jnp.int32)
    matching = owner_ids[:, None] == owner_ids[None, :]
    earlier = positions[None, :] < positions[:, None]
    slot_rank = jnp.sum(jnp.logical_and(matching, earlier).astype(jnp.int32), axis=1)
    target = owner_ids * CAP + slot_rank
    slots = jnp.arange(girth_count * CAP, dtype=jnp.int32)
    hit = target[None, :] == slots[:, None]
    filled = jnp.any(hit, axis=1)
    slot_row = jnp.sum(jnp.where(hit, tile_ids[None, :], 0), axis=1)
    stiffness_at = jnp.take(stiffness, slot_row, axis=0)
    motion_at = jnp.take(motion, slot_row, axis=1)
    stress_rows = stiffness_at[:, None, :] * jnp.einsum(
        "ka,aij->ikj", stress_map, motion_at, precision=lax.Precision.HIGHEST
    )
    spectra = square_pairs(stress_rows, 1)
    outbox = jnp.where(filled[:, None, None], spectra, 0.0)
    outbox = outbox.reshape(girth_count, CAP * 2 * girth_cells // 128, 128)
    received = lax.all_to_all(outbox, "girth", split_axis=0, concat_axis=0, tiled=True)
    received = received.reshape(girth_count, CAP, 2, girth_cells)
    hotspot_moments = prior_moments + (psd_weight[0] * received)[None, None]
    return (motion, hotspot_moments)


def solution(mesh):
    return jax.shard_map(
        on_device,
        mesh=mesh,
        in_specs=(
            P(None, "length", "girth"),
            P("girth", None),
            P(),
            P("length", "girth"),
            P(),
            P(),
            P(),
            P(),
            P("length", "girth"),
            P("length", "girth", None),
            P("length", "girth", None, None, None, None),
        ),
        out_specs=(P(None, "length", "girth"), P("length", "girth", None, None, None, None)),
        check_vma=False,
    )
```

```python
import math

import jax
import jax.numpy as jnp
from jax import lax
from jax.sharding import PartitionSpec as P

SWEEPS = 4
CAP = 2


def scatter_gather(block, axis, source):
    count = lax.axis_size(axis)
    rows = block.shape[0]
    send = block.reshape(count, rows // count, block.shape[1])
    got = lax.all_to_all(send, axis, 0, 0, tiled=True)
    mine = lax.dynamic_index_in_dim(got, source, 0, keepdims=False)
    send = jnp.broadcast_to(mine[None], (count,) + mine.shape)
    full = lax.all_to_all(send, axis, 0, 0, tiled=True)
    return full.reshape(rows, block.shape[1])


def spread(block, axis, source, pair_axis):
    core = lax.axis_index(pair_axis) % 2
    half = block.shape[0] // 2
    mine = lax.dynamic_slice_in_dim(block, core * half, half, 0)
    got = scatter_gather(mine, axis, source)
    pairs = [(i, i ^ 1) for i in range(lax.axis_size(pair_axis))]
    other = lax.ppermute(got, pair_axis, pairs)
    low = jnp.where(core == 0, got, other)
    high = jnp.where(core == 0, other, got)
    return jnp.concatenate([low, high], axis=0)


def padded_2(block, sides, width):
    for axis, dim in sides:
        count = lax.axis_size(axis)
        forward = [(i, i + 1) for i in range(count - 1)]
        backward = [(target, source) for source, target in forward]
        low = lax.ppermute(
            lax.slice_in_dim(block, block.shape[dim] - width, None, axis=dim), axis, forward
        )
        high = lax.ppermute(lax.slice_in_dim(block, 0, width, axis=dim), axis, backward)
        block = jnp.concatenate([low, block, high], axis=dim)
    return block


def padded_last(block, axis, width):
    count = lax.axis_size(axis)
    forward = [(i, i + 1) for i in range(count - 1)]
    backward = [(target, source) for source, target in forward]
    lead, rows = block.shape[0], block.shape[1]

    def pack(strip):
        return jnp.swapaxes(strip, 1, 2).reshape(lead * width, rows)

    def unpack(flat):
        return jnp.swapaxes(flat.reshape(lead, width, rows), 1, 2)

    low = unpack(lax.ppermute(pack(block[:, :, block.shape[2] - width :]), axis, forward))
    high = unpack(lax.ppermute(pack(block[:, :, :width]), axis, backward))
    return jnp.concatenate([low, block, high], axis=2)


def chebyshev_weight(sweep):
    return 1.0 / (1.0 + 0.9 * math.cos(math.pi * (2 * sweep + 1) / (2 * SWEEPS)))


def operate_padded(padded, stiffness, coupling):
    centre = padded[:, 1:-1, 1:-1]
    beside = padded[:, 2:, 1:-1] + padded[:, :-2, 1:-1] + padded[:, 1:-1, 2:] + padded[:, 1:-1, :-2]
    fields = centre.shape[0]
    mixing = [sum(coupling[a, b] * centre[b] for b in range(fields)) for a in range(fields)]
    return stiffness * (4.0 * centre - beside) + jnp.stack(mixing)


def square_pairs(values, axis_at):
    first = jnp.take(values, 0, axis=axis_at)
    second = jnp.take(values, 1, axis=axis_at)
    third = jnp.take(values, 2, axis=axis_at)
    fourth = jnp.take(values, 3, axis=axis_at)
    return jnp.stack(
        [first * first + second * second, third * third + fourth * fourth], axis=axis_at
    )


def on_device(
    wave_amplitude,
    load_bank,
    freq_owner,
    thickness_class,
    class_stiffness,
    coupling,
    stress_map,
    psd_weight,
    hotspot_tile,
    hotspot_owner,
    prior_moments,
):
    row_count = wave_amplitude.shape[1]
    girth_cells = load_bank.shape[1]
    mode_count = load_bank.shape[0]
    width = SWEEPS - 1
    root = freq_owner[0]
    stiffness = jnp.zeros((row_count, girth_cells), jnp.float32)
    for level in range(class_stiffness.shape[0]):
        stiffness = stiffness + jnp.where(thickness_class == level, class_stiffness[level], 0.0)
    amplitude_ext = padded_2(wave_amplitude, (("length", 1),), width)
    stiffness_rows = padded_2(stiffness, (("length", 0),), width)
    factors = spread(load_bank, "girth", root, "length")
    ext_rows = row_count + 2 * width
    loading = jnp.dot(amplitude_ext.reshape(6 * ext_rows, mode_count), factors, preferred_element_type=jnp.float32)
    loading = loading.reshape(6, ext_rows, girth_cells)
    coupling_diag = jnp.diagonal(coupling)[:, None, None]
    packed = jnp.concatenate([loading, stiffness_rows[None]], axis=0)
    packed = padded_last(packed, "girth", width)
    loading_ext = packed[:6]
    stiffness_ext = packed[6]
    diagonal_ext = 4.0 * stiffness_ext[None] + coupling_diag
    motion = chebyshev_weight(0) * (loading_ext / diagonal_ext)
    for sweep in range(1, SWEEPS):
        applied = operate_padded(motion, stiffness_ext[1:-1, 1:-1], coupling)
        loading_ext = loading_ext[:, 1:-1, 1:-1]
        stiffness_ext = stiffness_ext[1:-1, 1:-1]
        diagonal_ext = diagonal_ext[:, 1:-1, 1:-1]
        motion = motion[:, 1:-1, 1:-1] + chebyshev_weight(sweep) * ((loading_ext - applied) / diagonal_ext)
    girth_count = lax.axis_size("girth")
    tile_ids = hotspot_tile[0]
    owner_ids = hotspot_owner[0, :, 0]
    listed = owner_ids.shape[0]
    positions = jnp.arange(listed, dtype=jnp.int32)
    matching = owner_ids[:, None] == owner_ids[None, :]
    earlier = positions[None, :] < positions[:, None]
    slot_rank = jnp.sum(jnp.logical_and(matching, earlier).astype(jnp.int32), axis=1)
    target = owner_ids * CAP + slot_rank
    slots = jnp.arange(girth_count * CAP, dtype=jnp.int32)
    hit = target[None, :] == slots[:, None]
    filled = jnp.any(hit, axis=1)
    slot_row = jnp.sum(jnp.where(hit, tile_ids[None, :], 0), axis=1)
    stiffness_at = jnp.take(stiffness, slot_row, axis=0)
    motion_at = jnp.take(motion, slot_row, axis=1)
    stress_rows = stiffness_at[:, None, :] * jnp.einsum(
        "ka,aij->ikj", stress_map, motion_at, precision=lax.Precision.HIGHEST
    )
    spectra = square_pairs(stress_rows, 1)
    outbox = jnp.where(filled[:, None, None], spectra, 0.0)
    outbox = outbox.reshape(girth_count, CAP * 2 * girth_cells // 128, 128)
    received = lax.all_to_all(outbox, "girth", split_axis=0, concat_axis=0, tiled=True)
    received = received.reshape(girth_count, CAP, 2, girth_cells)
    hotspot_moments = prior_moments + (psd_weight[0] * received)[None, None]
    return (motion, hotspot_moments)


def solution(mesh):
    return jax.shard_map(
        on_device,
        mesh=mesh,
        in_specs=(
            P(None, "length", "girth"),
            P("girth", None),
            P(),
            P("length", "girth"),
            P(),
            P(),
            P(),
            P(),
            P("length", "girth"),
            P("length", "girth", None),
            P("length", "girth", None, None, None, None),
        ),
        out_specs=(P(None, "length", "girth"), P("length", "girth", None, None, None, None)),
        check_vma=False,
    )
```

```python
import math

import jax
import jax.numpy as jnp
from jax import lax
from jax.sharding import PartitionSpec as P
from jax.experimental import pallas as pl
from jax.experimental.pallas import tpu as pltpu

SWEEPS = 4
CAP = 2


def scatter_gather(block, axis, source):
    count = lax.axis_size(axis)
    rows = block.shape[0]
    send = block.reshape(count, rows // count, block.shape[1])
    got = lax.all_to_all(send, axis, 0, 0, tiled=True)
    mine = lax.dynamic_index_in_dim(got, source, 0, keepdims=False)
    send = jnp.broadcast_to(mine[None], (count,) + mine.shape)
    full = lax.all_to_all(send, axis, 0, 0, tiled=True)
    return full.reshape(rows, block.shape[1])


def spread(block, axis, source, pair_axis):
    core = lax.axis_index(pair_axis) % 2
    half = block.shape[0] // 2
    mine = lax.dynamic_slice_in_dim(block, core * half, half, 0)
    got = scatter_gather(mine, axis, source)
    pairs = [(i, i ^ 1) for i in range(lax.axis_size(pair_axis))]
    other = lax.ppermute(got, pair_axis, pairs)
    low = jnp.where(core == 0, got, other)
    high = jnp.where(core == 0, other, got)
    return jnp.concatenate([low, high], axis=0)


def padded_2(block, sides, width):
    for axis, dim in sides:
        count = lax.axis_size(axis)
        forward = [(i, i + 1) for i in range(count - 1)]
        backward = [(target, source) for source, target in forward]
        low = lax.ppermute(
            lax.slice_in_dim(block, block.shape[dim] - width, None, axis=dim), axis, forward
        )
        high = lax.ppermute(lax.slice_in_dim(block, 0, width, axis=dim), axis, backward)
        block = jnp.concatenate([low, block, high], axis=dim)
    return block


def padded_last(block, axis, width):
    count = lax.axis_size(axis)
    forward = [(i, i + 1) for i in range(count - 1)]
    backward = [(target, source) for source, target in forward]
    lead, rows = block.shape[0], block.shape[1]

    def pack(strip):
        return jnp.swapaxes(strip, 1, 2).reshape(lead * width, rows)

    def unpack(flat):
        return jnp.swapaxes(flat.reshape(lead, width, rows), 1, 2)

    low = unpack(lax.ppermute(pack(block[:, :, block.shape[2] - width :]), axis, forward))
    high = unpack(lax.ppermute(pack(block[:, :, :width]), axis, backward))
    return jnp.concatenate([low, block, high], axis=2)


def sweeps_kernel(coupling_ref, packed_ref, out_ref, motion_ref, next_ref):
    fields = out_ref.shape[0]
    rows, cols = packed_ref.shape[1], packed_ref.shape[2]
    width = SWEEPS - 1
    stiffness = packed_ref[fields]
    for a in range(fields):
        diagonal = 4.0 * stiffness + coupling_ref[a * fields + a]
        motion_ref[a] = chebyshev_weight(0) * (packed_ref[a] / diagonal)
    source, target = motion_ref, next_ref
    for sweep in range(1, SWEEPS):
        for a in range(fields):
            centre = source[a]
            beside = (
                pltpu.roll(centre, rows - 1, 0)
                + pltpu.roll(centre, 1, 0)
                + pltpu.roll(centre, cols - 1, 1)
                + pltpu.roll(centre, 1, 1)
            )
            mixing = coupling_ref[a * fields] * source[0]
            for b in range(1, fields):
                mixing = mixing + coupling_ref[a * fields + b] * source[b]
            applied = stiffness * (4.0 * centre - beside) + mixing
            diagonal = 4.0 * stiffness + coupling_ref[a * fields + a]
            target[a] = centre + chebyshev_weight(sweep) * ((packed_ref[a] - applied) / diagonal)
        source, target = target, source
    out_rows, out_cols = out_ref.shape[1], out_ref.shape[2]
    for a in range(fields):
        moved = pltpu.roll(pltpu.roll(source[a], rows - width, 0), cols - width, 1)
        out_ref[a] = moved[:out_rows, :out_cols]


def run_sweeps(packed, coupling, out_rows, out_cols):
    fields = packed.shape[0] - 1
    return pl.pallas_call(
        sweeps_kernel,
        out_shape=jax.ShapeDtypeStruct((fields, out_rows, out_cols), jnp.float32),
        in_specs=[
            pl.BlockSpec(memory_space=pltpu.SMEM),
            pl.BlockSpec(memory_space=pltpu.VMEM),
        ],
        out_specs=pl.BlockSpec(memory_space=pltpu.VMEM),
        scratch_shapes=[pltpu.VMEM((fields,) + packed.shape[1:], jnp.float32)] * 2,
    )(coupling.reshape(-1), packed)


def chebyshev_weight(sweep):
    return 1.0 / (1.0 + 0.9 * math.cos(math.pi * (2 * sweep + 1) / (2 * SWEEPS)))


def operate_padded(padded, stiffness, coupling):
    centre = padded[:, 1:-1, 1:-1]
    beside = padded[:, 2:, 1:-1] + padded[:, :-2, 1:-1] + padded[:, 1:-1, 2:] + padded[:, 1:-1, :-2]
    mixing = jnp.einsum("ab,bij->aij", coupling, centre, precision=lax.Precision.HIGHEST)
    return stiffness * (4.0 * centre - beside) + mixing


def square_pairs(values, axis_at):
    first = jnp.take(values, 0, axis=axis_at)
    second = jnp.take(values, 1, axis=axis_at)
    third = jnp.take(values, 2, axis=axis_at)
    fourth = jnp.take(values, 3, axis=axis_at)
    return jnp.stack(
        [first * first + second * second, third * third + fourth * fourth], axis=axis_at
    )


def on_device(
    wave_amplitude,
    load_bank,
    freq_owner,
    thickness_class,
    class_stiffness,
    coupling,
    stress_map,
    psd_weight,
    hotspot_tile,
    hotspot_owner,
    prior_moments,
):
    row_count = wave_amplitude.shape[1]
    girth_cells = load_bank.shape[1]
    mode_count = load_bank.shape[0]
    width = SWEEPS - 1
    root = freq_owner[0]
    stiffness = jnp.zeros((row_count, girth_cells), jnp.float32)
    for level in range(class_stiffness.shape[0]):
        stiffness = stiffness + jnp.where(thickness_class == level, class_stiffness[level], 0.0)
    amplitude_ext = padded_2(wave_amplitude, (("length", 1),), width)
    stiffness_rows = padded_2(stiffness, (("length", 0),), width)
    factors = spread(load_bank, "girth", root, "length")
    ext_rows = row_count + 2 * width
    loading = jnp.dot(amplitude_ext.reshape(6 * ext_rows, mode_count), factors, preferred_element_type=jnp.float32)
    loading = loading.reshape(6, ext_rows, girth_cells)
    coupling_diag = jnp.diagonal(coupling)[:, None, None]
    packed = jnp.concatenate([loading, stiffness_rows[None]], axis=0)
    packed = padded_last(packed, "girth", width)
    ext_cols = packed.shape[2]
    packed = jnp.pad(packed, ((0, 0), (0, -ext_rows % 8), (0, -ext_cols % 128)))
    motion = run_sweeps(packed, coupling, row_count, girth_cells)
    girth_count = lax.axis_size("girth")
    tile_ids = hotspot_tile[0]
    owner_ids = hotspot_owner[0, :, 0]
    listed = owner_ids.shape[0]
    positions = jnp.arange(listed, dtype=jnp.int32)
    matching = owner_ids[:, None] == owner_ids[None, :]
    earlier = positions[None, :] < positions[:, None]
    slot_rank = jnp.sum(jnp.logical_and(matching, earlier).astype(jnp.int32), axis=1)
    target = owner_ids * CAP + slot_rank
    slots = jnp.arange(girth_count * CAP, dtype=jnp.int32)
    hit = target[None, :] == slots[:, None]
    filled = jnp.any(hit, axis=1)
    slot_row = jnp.sum(jnp.where(hit, tile_ids[None, :], 0), axis=1)
    stiffness_at = jnp.take(stiffness, slot_row, axis=0)
    motion_at = jnp.take(motion, slot_row, axis=1)
    stress_rows = stiffness_at[:, None, :] * jnp.einsum(
        "ka,aij->ikj", stress_map, motion_at, precision=lax.Precision.HIGHEST
    )
    spectra = square_pairs(stress_rows, 1)
    outbox = jnp.where(filled[:, None, None], spectra, 0.0)
    outbox = outbox.reshape(girth_count, CAP * 2 * girth_cells // 128, 128)
    received = lax.all_to_all(outbox, "girth", split_axis=0, concat_axis=0, tiled=True)
    received = received.reshape(girth_count, CAP, 2, girth_cells)
    hotspot_moments = prior_moments + (psd_weight[0] * received)[None, None]
    return (motion, hotspot_moments)


def solution(mesh):
    return jax.shard_map(
        on_device,
        mesh=mesh,
        in_specs=(
            P(None, "length", "girth"),
            P("girth", None),
            P(),
            P("length", "girth"),
            P(),
            P(),
            P(),
            P(),
            P("length", "girth"),
            P("length", "girth", None),
            P("length", "girth", None, None, None, None),
        ),
        out_specs=(P(None, "length", "girth"), P("length", "girth", None, None, None, None)),
        check_vma=False,
    )
```

```python
import math

import jax
import jax.numpy as jnp
from jax import lax
from jax.sharding import PartitionSpec as P
from jax.experimental import pallas as pl
from jax.experimental.pallas import tpu as pltpu

SWEEPS = 4
CAP = 2


def scatter_gather(block, axis, source):
    count = lax.axis_size(axis)
    rows = block.shape[0]
    send = block.reshape(count, rows // count, block.shape[1])
    got = lax.all_to_all(send, axis, 0, 0, tiled=True)
    mine = lax.dynamic_index_in_dim(got, source, 0, keepdims=False)
    send = jnp.broadcast_to(mine[None], (count,) + mine.shape)
    full = lax.all_to_all(send, axis, 0, 0, tiled=True)
    return full.reshape(rows, block.shape[1])


def spread(block, axis, source, pair_axis):
    core = lax.axis_index(pair_axis) % 2
    half = block.shape[0] // 2
    mine = lax.dynamic_slice_in_dim(block, core * half, half, 0)
    got = scatter_gather(mine, axis, source)
    pairs = [(i, i ^ 1) for i in range(lax.axis_size(pair_axis))]
    other = lax.ppermute(got, pair_axis, pairs)
    low = jnp.where(core == 0, got, other)
    high = jnp.where(core == 0, other, got)
    return jnp.concatenate([low, high], axis=0)


def padded_2(block, sides, width):
    for axis, dim in sides:
        count = lax.axis_size(axis)
        forward = [(i, i + 1) for i in range(count - 1)]
        backward = [(target, source) for source, target in forward]
        low = lax.ppermute(
            lax.slice_in_dim(block, block.shape[dim] - width, None, axis=dim), axis, forward
        )
        high = lax.ppermute(lax.slice_in_dim(block, 0, width, axis=dim), axis, backward)
        block = jnp.concatenate([low, block, high], axis=dim)
    return block


def padded_last(block, axis, width):
    count = lax.axis_size(axis)
    forward = [(i, i + 1) for i in range(count - 1)]
    backward = [(target, source) for source, target in forward]
    lead, rows = block.shape[0], block.shape[1]

    def pack(strip):
        return jnp.swapaxes(strip, 1, 2).reshape(lead * width, rows)

    def unpack(flat):
        return jnp.swapaxes(flat.reshape(lead, width, rows), 1, 2)

    low = unpack(lax.ppermute(pack(block[:, :, block.shape[2] - width :]), axis, forward))
    high = unpack(lax.ppermute(pack(block[:, :, :width]), axis, backward))
    return jnp.concatenate([low, block, high], axis=2)


def sweeps_kernel(
    rows_ref, coupling_ref, loading_ref, side_ref, stiff_ref, stiff_side_ref,
    out_ref, picked_ref, load_scr, stiff_scr, motion_ref, next_ref,
):
    fields = out_ref.shape[0]
    cells = loading_ref.shape[2]
    rows, cols = load_scr.shape[1], load_scr.shape[2]
    stiff_scr[:, :cells] = stiff_ref[...]
    stiff_scr[:, cells:] = stiff_side_ref[...]
    for a in range(fields):
        load_scr[a, :, :cells] = loading_ref[a]
        load_scr[a, :, cells:] = side_ref[a]
    stiffness = stiff_scr[...]
    for a in range(fields):
        diagonal = 4.0 * stiffness + coupling_ref[a, a]
        motion_ref[a] = chebyshev_weight(0) * (load_scr[a] / diagonal)
    source, target = motion_ref, next_ref
    for sweep in range(1, SWEEPS):
        for a in range(fields):
            centre = source[a]
            beside = (
                pltpu.roll(centre, rows - 1, 0)
                + pltpu.roll(centre, 1, 0)
                + pltpu.roll(centre, cols - 1, 1)
                + pltpu.roll(centre, 1, 1)
            )
            mixing = coupling_ref[a, 0] * source[0]
            for b in range(1, fields):
                mixing = mixing + coupling_ref[a, b] * source[b]
            applied = stiffness * (4.0 * centre - beside) + mixing
            diagonal = 4.0 * stiffness + coupling_ref[a, a]
            target[a] = centre + chebyshev_weight(sweep) * ((load_scr[a] - applied) / diagonal)
        source, target = target, source
    out_rows = out_ref.shape[1]
    for a in range(fields):
        out_ref[a] = source[a, :out_rows, :cells]
    for slot in range(picked_ref.shape[1]):
        row = rows_ref[slot]
        for a in range(fields):
            picked_ref[a, pl.ds(slot, 1), :] = source[a, pl.ds(row, 1), pl.ds(0, cells)]


def run_sweeps(slot_row, coupling, loading, side, stiffness, stiffness_side, out_rows):
    fields, rows, cells = loading.shape
    cols = cells + side.shape[2]
    smem = pl.BlockSpec(memory_space=pltpu.SMEM)
    vmem = pl.BlockSpec(memory_space=pltpu.VMEM)
    return pl.pallas_call(
        sweeps_kernel,
        out_shape=(
            jax.ShapeDtypeStruct((fields, out_rows, cells), jnp.float32),
            jax.ShapeDtypeStruct((fields, slot_row.shape[0], cells), jnp.float32),
        ),
        in_specs=[smem, smem, vmem, vmem, vmem, vmem],
        out_specs=(vmem, vmem),
        scratch_shapes=[
            pltpu.VMEM((fields, rows, cols), jnp.float32),
            pltpu.VMEM((rows, cols), jnp.float32),
            pltpu.VMEM((fields, rows, cols), jnp.float32),
            pltpu.VMEM((fields, rows, cols), jnp.float32),
        ],
    )(slot_row, coupling, loading, side, stiffness, stiffness_side)


def cyclic_rows(block, axis, dim, width, rows):
    count = lax.axis_size(axis)
    forward = [(i, i + 1) for i in range(count - 1)]
    backward = [(target, source) for source, target in forward]
    size = block.shape[dim]
    before = lax.ppermute(lax.slice_in_dim(block, size - width, None, axis=dim), axis, forward)
    after = lax.ppermute(lax.slice_in_dim(block, 0, width, axis=dim), axis, backward)
    gap_shape = list(block.shape)
    gap_shape[dim] = rows - size - 2 * width
    return jnp.concatenate([block, after, jnp.zeros(gap_shape, block.dtype), before], axis=dim)


def cyclic_side(block, axis, width, lanes):
    count = lax.axis_size(axis)
    forward = [(i, i + 1) for i in range(count - 1)]
    backward = [(target, source) for source, target in forward]
    lead, rows = block.shape[0], block.shape[1]

    def pack(strip):
        return jnp.swapaxes(strip, 1, 2).reshape(lead * width, rows)

    def unpack(flat):
        return jnp.swapaxes(flat.reshape(lead, width, rows), 1, 2)

    before = unpack(lax.ppermute(pack(block[:, :, block.shape[2] - width :]), axis, forward))
    after = unpack(lax.ppermute(pack(block[:, :, :width]), axis, backward))
    gap = jnp.zeros((lead, rows, lanes - 2 * width), block.dtype)
    return jnp.concatenate([after, gap, before], axis=2)


def chebyshev_weight(sweep):
    return 1.0 / (1.0 + 0.9 * math.cos(math.pi * (2 * sweep + 1) / (2 * SWEEPS)))


def operate_padded(padded, stiffness, coupling):
    centre = padded[:, 1:-1, 1:-1]
    beside = padded[:, 2:, 1:-1] + padded[:, :-2, 1:-1] + padded[:, 1:-1, 2:] + padded[:, 1:-1, :-2]
    mixing = jnp.einsum("ab,bij->aij", coupling, centre, precision=lax.Precision.HIGHEST)
    return stiffness * (4.0 * centre - beside) + mixing


def square_pairs(values, axis_at):
    first = jnp.take(values, 0, axis=axis_at)
    second = jnp.take(values, 1, axis=axis_at)
    third = jnp.take(values, 2, axis=axis_at)
    fourth = jnp.take(values, 3, axis=axis_at)
    return jnp.stack(
        [first * first + second * second, third * third + fourth * fourth], axis=axis_at
    )


def on_device(
    wave_amplitude,
    load_bank,
    freq_owner,
    thickness_class,
    class_stiffness,
    coupling,
    stress_map,
    psd_weight,
    hotspot_tile,
    hotspot_owner,
    prior_moments,
):
    row_count = wave_amplitude.shape[1]
    girth_cells = load_bank.shape[1]
    mode_count = load_bank.shape[0]
    width = SWEEPS - 1
    root = freq_owner[0]
    stiffness = jnp.zeros((row_count, girth_cells), jnp.float32)
    for level in range(class_stiffness.shape[0]):
        stiffness = stiffness + jnp.where(thickness_class == level, class_stiffness[level], 0.0)
    ring_rows = -(-(row_count + 2 * width) // 8) * 8
    amplitude_ext = cyclic_rows(wave_amplitude, "length", 1, width, ring_rows)
    stiffness_ext = cyclic_rows(stiffness, "length", 0, width, ring_rows)
    stiffness_side = cyclic_side(stiffness_ext[None], "girth", width, 128)[0]
    girth_count = lax.axis_size("girth")
    tile_ids = hotspot_tile[0]
    owner_ids = hotspot_owner[0, :, 0]
    listed = owner_ids.shape[0]
    positions = jnp.arange(listed, dtype=jnp.int32)
    matching = owner_ids[:, None] == owner_ids[None, :]
    earlier = positions[None, :] < positions[:, None]
    slot_rank = jnp.sum(jnp.logical_and(matching, earlier).astype(jnp.int32), axis=1)
    target = owner_ids * CAP + slot_rank
    slots = jnp.arange(girth_count * CAP, dtype=jnp.int32)
    hit = target[None, :] == slots[:, None]
    filled = jnp.any(hit, axis=1)
    slot_row = jnp.sum(jnp.where(hit, tile_ids[None, :], 0), axis=1)
    stiffness_at = jnp.take(stiffness, slot_row, axis=0)
    factors = spread(load_bank, "girth", root, "length")
    loading = jnp.dot(amplitude_ext.reshape(6 * ring_rows, mode_count), factors, preferred_element_type=jnp.float32)
    loading = loading.reshape(6, ring_rows, girth_cells)
    loading_side = cyclic_side(loading, "girth", width, 128)
    motion, motion_at = run_sweeps(
        slot_row, coupling, loading, loading_side, stiffness_ext, stiffness_side, row_count
    )
    stress_rows = stiffness_at[:, None, :] * jnp.einsum(
        "ka,aij->ikj", stress_map, motion_at, precision=lax.Precision.HIGHEST
    )
    spectra = square_pairs(stress_rows, 1)
    outbox = jnp.where(filled[:, None, None], spectra, 0.0)
    outbox = outbox.reshape(girth_count, CAP * 2 * girth_cells // 128, 128)
    received = lax.all_to_all(outbox, "girth", split_axis=0, concat_axis=0, tiled=True)
    received = received.reshape(girth_count, CAP, 2, girth_cells)
    hotspot_moments = prior_moments + (psd_weight[0] * received)[None, None]
    return (motion, hotspot_moments)


def solution(mesh):
    return jax.shard_map(
        on_device,
        mesh=mesh,
        in_specs=(
            P(None, "length", "girth"),
            P("girth", None),
            P(),
            P("length", "girth"),
            P(),
            P(),
            P(),
            P(),
            P("length", "girth"),
            P("length", "girth", None),
            P("length", "girth", None, None, None, None),
        ),
        out_specs=(P(None, "length", "girth"), P("length", "girth", None, None, None, None)),
        check_vma=False,
    )
```

```python
import math

import jax
import jax.numpy as jnp
from jax import lax
from jax.sharding import PartitionSpec as P
from jax.experimental import pallas as pl
from jax.experimental.pallas import tpu as pltpu

SWEEPS = 4
CAP = 2


def scatter_gather(block, axis, source):
    count = lax.axis_size(axis)
    rows = block.shape[0]
    send = block.reshape(count, rows // count, block.shape[1])
    got = lax.all_to_all(send, axis, 0, 0, tiled=True)
    mine = lax.dynamic_index_in_dim(got, source, 0, keepdims=False)
    send = jnp.broadcast_to(mine[None], (count,) + mine.shape)
    full = lax.all_to_all(send, axis, 0, 0, tiled=True)
    return full.reshape(rows, block.shape[1])


def spread(block, axis, source, pair_axis):
    core = lax.axis_index(pair_axis) % 2
    half = block.shape[0] // 2
    mine = lax.dynamic_slice_in_dim(block, core * half, half, 0)
    got = scatter_gather(mine, axis, source)
    pairs = [(i, i ^ 1) for i in range(lax.axis_size(pair_axis))]
    other = lax.ppermute(got, pair_axis, pairs)
    low = jnp.where(core == 0, got, other)
    high = jnp.where(core == 0, other, got)
    return jnp.concatenate([low, high], axis=0)


def padded_2(block, sides, width):
    for axis, dim in sides:
        count = lax.axis_size(axis)
        forward = [(i, i + 1) for i in range(count - 1)]
        backward = [(target, source) for source, target in forward]
        low = lax.ppermute(
            lax.slice_in_dim(block, block.shape[dim] - width, None, axis=dim), axis, forward
        )
        high = lax.ppermute(lax.slice_in_dim(block, 0, width, axis=dim), axis, backward)
        block = jnp.concatenate([low, block, high], axis=dim)
    return block


def padded_last(block, axis, width):
    count = lax.axis_size(axis)
    forward = [(i, i + 1) for i in range(count - 1)]
    backward = [(target, source) for source, target in forward]
    lead, rows = block.shape[0], block.shape[1]

    def pack(strip):
        return jnp.swapaxes(strip, 1, 2).reshape(lead * width, rows)

    def unpack(flat):
        return jnp.swapaxes(flat.reshape(lead, width, rows), 1, 2)

    low = unpack(lax.ppermute(pack(block[:, :, block.shape[2] - width :]), axis, forward))
    high = unpack(lax.ppermute(pack(block[:, :, :width]), axis, backward))
    return jnp.concatenate([low, block, high], axis=2)


def sweeps_kernel(
    rows_ref, coupling_ref, loading_ref, side_ref, stiff_ref,
    out_ref, picked_ref, load_scr, stiff_scr, motion_ref, next_ref,
):
    fields = out_ref.shape[0]
    cells = loading_ref.shape[2]
    rows, cols = load_scr.shape[1], load_scr.shape[2]
    stiff_scr[:, :cells] = stiff_ref[...]
    stiff_scr[:, cells:] = side_ref[fields]
    for a in range(fields):
        load_scr[a, :, :cells] = loading_ref[a]
        load_scr[a, :, cells:] = side_ref[a]
    stiffness = stiff_scr[...]
    for a in range(fields):
        diagonal = 4.0 * stiffness + coupling_ref[a, a]
        motion_ref[a] = chebyshev_weight(0) * (load_scr[a] / diagonal)
    source, target = motion_ref, next_ref
    for sweep in range(1, SWEEPS):
        for a in range(fields):
            centre = source[a]
            beside = (
                pltpu.roll(centre, rows - 1, 0)
                + pltpu.roll(centre, 1, 0)
                + pltpu.roll(centre, cols - 1, 1)
                + pltpu.roll(centre, 1, 1)
            )
            mixing = coupling_ref[a, 0] * source[0]
            for b in range(1, fields):
                mixing = mixing + coupling_ref[a, b] * source[b]
            applied = stiffness * (4.0 * centre - beside) + mixing
            diagonal = 4.0 * stiffness + coupling_ref[a, a]
            target[a] = centre + chebyshev_weight(sweep) * ((load_scr[a] - applied) / diagonal)
        source, target = target, source
    out_rows = out_ref.shape[1]
    for a in range(fields):
        out_ref[a] = source[a, :out_rows, :cells]
    for slot in range(picked_ref.shape[1]):
        row = rows_ref[slot]
        for a in range(fields):
            picked_ref[a, pl.ds(slot, 1), :] = source[a, pl.ds(row, 1), pl.ds(0, cells)]


def run_sweeps(slot_row, coupling, loading, side, stiffness, out_rows):
    fields, rows, cells = loading.shape
    cols = cells + side.shape[2]
    smem = pl.BlockSpec(memory_space=pltpu.SMEM)
    vmem = pl.BlockSpec(memory_space=pltpu.VMEM)
    return pl.pallas_call(
        sweeps_kernel,
        out_shape=(
            jax.ShapeDtypeStruct((fields, out_rows, cells), jnp.float32),
            jax.ShapeDtypeStruct((fields, slot_row.shape[0], cells), jnp.float32),
        ),
        in_specs=[smem, smem, vmem, vmem, vmem],
        out_specs=(vmem, vmem),
        scratch_shapes=[
            pltpu.VMEM((fields, rows, cols), jnp.float32),
            pltpu.VMEM((rows, cols), jnp.float32),
            pltpu.VMEM((fields, rows, cols), jnp.float32),
            pltpu.VMEM((fields, rows, cols), jnp.float32),
        ],
    )(slot_row, coupling, loading, side, stiffness)


def cyclic_rows(block, axis, dim, width, rows):
    count = lax.axis_size(axis)
    forward = [(i, i + 1) for i in range(count - 1)]
    backward = [(target, source) for source, target in forward]
    size = block.shape[dim]
    before = lax.ppermute(lax.slice_in_dim(block, size - width, None, axis=dim), axis, forward)
    after = lax.ppermute(lax.slice_in_dim(block, 0, width, axis=dim), axis, backward)
    gap_shape = list(block.shape)
    gap_shape[dim] = rows - size - 2 * width
    return jnp.concatenate([block, after, jnp.zeros(gap_shape, block.dtype), before], axis=dim)


def cyclic_side(blocks, axis, width, lanes):
    count = lax.axis_size(axis)
    forward = [(i, i + 1) for i in range(count - 1)]
    backward = [(target, source) for source, target in forward]
    lead = sum(block.shape[0] for block in blocks)
    rows = blocks[0].shape[1]
    size = blocks[0].shape[2]

    def pack(start):
        strip = jnp.concatenate([block[:, :, start : start + width] for block in blocks], axis=0)
        return jnp.swapaxes(strip, 1, 2).reshape(lead * width, rows)

    def unpack(flat):
        return jnp.swapaxes(flat.reshape(lead, width, rows), 1, 2)

    before = unpack(lax.ppermute(pack(size - width), axis, forward))
    after = unpack(lax.ppermute(pack(0), axis, backward))
    gap = jnp.zeros((lead, rows, lanes - 2 * width), before.dtype)
    return jnp.concatenate([after, gap, before], axis=2)


def chebyshev_weight(sweep):
    return 1.0 / (1.0 + 0.9 * math.cos(math.pi * (2 * sweep + 1) / (2 * SWEEPS)))


def operate_padded(padded, stiffness, coupling):
    centre = padded[:, 1:-1, 1:-1]
    beside = padded[:, 2:, 1:-1] + padded[:, :-2, 1:-1] + padded[:, 1:-1, 2:] + padded[:, 1:-1, :-2]
    mixing = jnp.einsum("ab,bij->aij", coupling, centre, precision=lax.Precision.HIGHEST)
    return stiffness * (4.0 * centre - beside) + mixing


def square_pairs(values, axis_at):
    first = jnp.take(values, 0, axis=axis_at)
    second = jnp.take(values, 1, axis=axis_at)
    third = jnp.take(values, 2, axis=axis_at)
    fourth = jnp.take(values, 3, axis=axis_at)
    return jnp.stack(
        [first * first + second * second, third * third + fourth * fourth], axis=axis_at
    )


def on_device(
    wave_amplitude,
    load_bank,
    freq_owner,
    thickness_class,
    class_stiffness,
    coupling,
    stress_map,
    psd_weight,
    hotspot_tile,
    hotspot_owner,
    prior_moments,
):
    row_count = wave_amplitude.shape[1]
    girth_cells = load_bank.shape[1]
    mode_count = load_bank.shape[0]
    width = SWEEPS - 1
    root = freq_owner[0]
    stiffness = jnp.zeros((row_count, girth_cells), jnp.float32)
    for level in range(class_stiffness.shape[0]):
        stiffness = stiffness + jnp.where(thickness_class == level, class_stiffness[level], 0.0)
    ring_rows = -(-(row_count + 2 * width) // 8) * 8
    amplitude_ext = cyclic_rows(wave_amplitude, "length", 1, width, ring_rows)
    stiffness_ext = cyclic_rows(stiffness, "length", 0, width, ring_rows)
    girth_count = lax.axis_size("girth")
    tile_ids = hotspot_tile[0]
    owner_ids = hotspot_owner[0, :, 0]
    listed = owner_ids.shape[0]
    positions = jnp.arange(listed, dtype=jnp.int32)
    matching = owner_ids[:, None] == owner_ids[None, :]
    earlier = positions[None, :] < positions[:, None]
    slot_rank = jnp.sum(jnp.logical_and(matching, earlier).astype(jnp.int32), axis=1)
    target = owner_ids * CAP + slot_rank
    slots = jnp.arange(girth_count * CAP, dtype=jnp.int32)
    hit = target[None, :] == slots[:, None]
    filled = jnp.any(hit, axis=1)
    slot_row = jnp.sum(jnp.where(hit, tile_ids[None, :], 0), axis=1)
    stiffness_at = jnp.take(stiffness, slot_row, axis=0)
    factors = spread(load_bank, "girth", root, "length")
    loading = jnp.dot(amplitude_ext.reshape(6 * ring_rows, mode_count), factors, preferred_element_type=jnp.float32)
    loading = loading.reshape(6, ring_rows, girth_cells)
    side = cyclic_side([loading, stiffness_ext[None]], "girth", width, 128)
    motion, motion_at = run_sweeps(slot_row, coupling, loading, side, stiffness_ext, row_count)
    stress_rows = stiffness_at[:, None, :] * jnp.einsum(
        "ka,aij->ikj", stress_map, motion_at, precision=lax.Precision.HIGHEST
    )
    spectra = square_pairs(stress_rows, 1)
    outbox = jnp.where(filled[:, None, None], spectra, 0.0)
    outbox = outbox.reshape(girth_count, CAP * 2 * girth_cells // 128, 128)
    received = lax.all_to_all(outbox, "girth", split_axis=0, concat_axis=0, tiled=True)
    received = received.reshape(girth_count, CAP, 2, girth_cells)
    hotspot_moments = prior_moments + (psd_weight[0] * received)[None, None]
    return (motion, hotspot_moments)


def solution(mesh):
    return jax.shard_map(
        on_device,
        mesh=mesh,
        in_specs=(
            P(None, "length", "girth"),
            P("girth", None),
            P(),
            P("length", "girth"),
            P(),
            P(),
            P(),
            P(),
            P("length", "girth"),
            P("length", "girth", None),
            P("length", "girth", None, None, None, None),
        ),
        out_specs=(P(None, "length", "girth"), P("length", "girth", None, None, None, None)),
        check_vma=False,
    )
```

```python
import math

import jax
import jax.numpy as jnp
from jax import lax
from jax.sharding import PartitionSpec as P
from jax.experimental import pallas as pl
from jax.experimental.pallas import tpu as pltpu

SWEEPS = 4
CAP = 2


def scatter_gather(block, axis, source):
    count = lax.axis_size(axis)
    rows = block.shape[0]
    send = block.reshape(count, rows // count, block.shape[1])
    got = lax.all_to_all(send, axis, 0, 0, tiled=True)
    mine = lax.dynamic_index_in_dim(got, source, 0, keepdims=False)
    send = jnp.broadcast_to(mine[None], (count,) + mine.shape)
    full = lax.all_to_all(send, axis, 0, 0, tiled=True)
    return full.reshape(rows, block.shape[1])


def spread(block, axis, source, pair_axis):
    core = lax.axis_index(pair_axis) % 2
    half = block.shape[0] // 2
    mine = lax.dynamic_slice_in_dim(block, core * half, half, 0)
    got = scatter_gather(mine, axis, source)
    pairs = [(i, i ^ 1) for i in range(lax.axis_size(pair_axis))]
    other = lax.ppermute(got, pair_axis, pairs)
    low = jnp.where(core == 0, got, other)
    high = jnp.where(core == 0, other, got)
    return jnp.concatenate([low, high], axis=0)


def padded_2(block, sides, width):
    for axis, dim in sides:
        count = lax.axis_size(axis)
        forward = [(i, i + 1) for i in range(count - 1)]
        backward = [(target, source) for source, target in forward]
        low = lax.ppermute(
            lax.slice_in_dim(block, block.shape[dim] - width, None, axis=dim), axis, forward
        )
        high = lax.ppermute(lax.slice_in_dim(block, 0, width, axis=dim), axis, backward)
        block = jnp.concatenate([low, block, high], axis=dim)
    return block


def padded_last(block, axis, width):
    count = lax.axis_size(axis)
    forward = [(i, i + 1) for i in range(count - 1)]
    backward = [(target, source) for source, target in forward]
    lead, rows = block.shape[0], block.shape[1]

    def pack(strip):
        return jnp.swapaxes(strip, 1, 2).reshape(lead * width, rows)

    def unpack(flat):
        return jnp.swapaxes(flat.reshape(lead, width, rows), 1, 2)

    low = unpack(lax.ppermute(pack(block[:, :, block.shape[2] - width :]), axis, forward))
    high = unpack(lax.ppermute(pack(block[:, :, :width]), axis, backward))
    return jnp.concatenate([low, block, high], axis=2)


def sweeps_kernel(rows_ref, coupling_ref, packed_ref, out_ref, picked_ref, motion_ref, next_ref):
    fields = out_ref.shape[0]
    rows, cols = packed_ref.shape[1], packed_ref.shape[2]
    width = SWEEPS - 1
    stiffness = packed_ref[fields]
    for a in range(fields):
        diagonal = 4.0 * stiffness + coupling_ref[a, a]
        motion_ref[a] = chebyshev_weight(0) * (packed_ref[a] / diagonal)
    source, target = motion_ref, next_ref
    for sweep in range(1, SWEEPS):
        for a in range(fields):
            centre = source[a]
            beside = (
                pltpu.roll(centre, rows - 1, 0)
                + pltpu.roll(centre, 1, 0)
                + pltpu.roll(centre, cols - 1, 1)
                + pltpu.roll(centre, 1, 1)
            )
            mixing = coupling_ref[a, 0] * source[0]
            for b in range(1, fields):
                mixing = mixing + coupling_ref[a, b] * source[b]
            applied = stiffness * (4.0 * centre - beside) + mixing
            diagonal = 4.0 * stiffness + coupling_ref[a, a]
            target[a] = centre + chebyshev_weight(sweep) * ((packed_ref[a] - applied) / diagonal)
        source, target = target, source
    out_rows, out_cols = out_ref.shape[1], out_ref.shape[2]
    for a in range(fields):
        moved = pltpu.roll(pltpu.roll(source[a], rows - width, 0), cols - width, 1)
        out_ref[a] = moved[:out_rows, :out_cols]
    for slot in range(picked_ref.shape[1]):
        row = rows_ref[slot] + width
        for a in range(fields):
            line = source[a, pl.ds(row, 1), :]
            picked_ref[a, pl.ds(slot, 1), :] = pltpu.roll(line, cols - width, 1)[:, :out_cols]


def run_sweeps(slot_row, packed, coupling, out_rows, out_cols):
    fields = packed.shape[0] - 1
    return pl.pallas_call(
        sweeps_kernel,
        out_shape=(
            jax.ShapeDtypeStruct((fields, out_rows, out_cols), jnp.float32),
            jax.ShapeDtypeStruct((fields, slot_row.shape[0], out_cols), jnp.float32),
        ),
        in_specs=[
            pl.BlockSpec(memory_space=pltpu.SMEM),
            pl.BlockSpec(memory_space=pltpu.SMEM),
            pl.BlockSpec(memory_space=pltpu.VMEM),
        ],
        out_specs=(pl.BlockSpec(memory_space=pltpu.VMEM), pl.BlockSpec(memory_space=pltpu.VMEM)),
        scratch_shapes=[pltpu.VMEM((fields,) + packed.shape[1:], jnp.float32)] * 2,
    )(slot_row, coupling, packed)


def chebyshev_weight(sweep):
    return 1.0 / (1.0 + 0.9 * math.cos(math.pi * (2 * sweep + 1) / (2 * SWEEPS)))


def operate_padded(padded, stiffness, coupling):
    centre = padded[:, 1:-1, 1:-1]
    beside = padded[:, 2:, 1:-1] + padded[:, :-2, 1:-1] + padded[:, 1:-1, 2:] + padded[:, 1:-1, :-2]
    mixing = jnp.einsum("ab,bij->aij", coupling, centre, precision=lax.Precision.HIGHEST)
    return stiffness * (4.0 * centre - beside) + mixing


def square_pairs(values, axis_at):
    first = jnp.take(values, 0, axis=axis_at)
    second = jnp.take(values, 1, axis=axis_at)
    third = jnp.take(values, 2, axis=axis_at)
    fourth = jnp.take(values, 3, axis=axis_at)
    return jnp.stack(
        [first * first + second * second, third * third + fourth * fourth], axis=axis_at
    )


def on_device(
    wave_amplitude,
    load_bank,
    freq_owner,
    thickness_class,
    class_stiffness,
    coupling,
    stress_map,
    psd_weight,
    hotspot_tile,
    hotspot_owner,
    prior_moments,
):
    row_count = wave_amplitude.shape[1]
    girth_cells = load_bank.shape[1]
    mode_count = load_bank.shape[0]
    width = SWEEPS - 1
    root = freq_owner[0]
    stiffness = jnp.zeros((row_count, girth_cells), jnp.float32)
    for level in range(class_stiffness.shape[0]):
        stiffness = stiffness + jnp.where(thickness_class == level, class_stiffness[level], 0.0)
    amplitude_ext = padded_2(wave_amplitude, (("length", 1),), width)
    stiffness_rows = padded_2(stiffness, (("length", 0),), width)
    factors = spread(load_bank, "girth", root, "length")
    ext_rows = row_count + 2 * width
    loading = jnp.dot(amplitude_ext.reshape(6 * ext_rows, mode_count), factors, preferred_element_type=jnp.float32)
    loading = loading.reshape(6, ext_rows, girth_cells)
    coupling_diag = jnp.diagonal(coupling)[:, None, None]
    packed = jnp.concatenate([loading, stiffness_rows[None]], axis=0)
    packed = padded_last(packed, "girth", width)
    girth_count = lax.axis_size("girth")
    tile_ids = hotspot_tile[0]
    owner_ids = hotspot_owner[0, :, 0]
    listed = owner_ids.shape[0]
    positions = jnp.arange(listed, dtype=jnp.int32)
    matching = owner_ids[:, None] == owner_ids[None, :]
    earlier = positions[None, :] < positions[:, None]
    slot_rank = jnp.sum(jnp.logical_and(matching, earlier).astype(jnp.int32), axis=1)
    target = owner_ids * CAP + slot_rank
    slots = jnp.arange(girth_count * CAP, dtype=jnp.int32)
    hit = target[None, :] == slots[:, None]
    filled = jnp.any(hit, axis=1)
    slot_row = jnp.sum(jnp.where(hit, tile_ids[None, :], 0), axis=1)
    stiffness_at = jnp.take(stiffness, slot_row, axis=0)
    ext_cols = packed.shape[2]
    packed = jnp.pad(packed, ((0, 0), (0, -ext_rows % 8), (0, -ext_cols % 128)))
    motion, motion_at = run_sweeps(slot_row, packed, coupling, row_count, girth_cells)
    stress_rows = stiffness_at[:, None, :] * jnp.einsum(
        "ka,aij->ikj", stress_map, motion_at, precision=lax.Precision.HIGHEST
    )
    spectra = square_pairs(stress_rows, 1)
    outbox = jnp.where(filled[:, None, None], spectra, 0.0)
    outbox = outbox.reshape(girth_count, CAP * 2 * girth_cells // 128, 128)
    received = lax.all_to_all(outbox, "girth", split_axis=0, concat_axis=0, tiled=True)
    received = received.reshape(girth_count, CAP, 2, girth_cells)
    hotspot_moments = prior_moments + (psd_weight[0] * received)[None, None]
    return (motion, hotspot_moments)


def solution(mesh):
    return jax.shard_map(
        on_device,
        mesh=mesh,
        in_specs=(
            P(None, "length", "girth"),
            P("girth", None),
            P(),
            P("length", "girth"),
            P(),
            P(),
            P(),
            P(),
            P("length", "girth"),
            P("length", "girth", None),
            P("length", "girth", None, None, None, None),
        ),
        out_specs=(P(None, "length", "girth"), P("length", "girth", None, None, None, None)),
        check_vma=False,
    )
```

```python
import math

import jax
import jax.numpy as jnp
from jax import lax
from jax.sharding import PartitionSpec as P
from jax.experimental import pallas as pl
from jax.experimental.pallas import tpu as pltpu

SWEEPS = 4
CAP = 2


def scatter_gather(block, axis, source):
    count = lax.axis_size(axis)
    rows = block.shape[0]
    send = block.reshape(count, rows // count, block.shape[1])
    got = lax.all_to_all(send, axis, 0, 0, tiled=True)
    mine = lax.dynamic_index_in_dim(got, source, 0, keepdims=False)
    send = jnp.broadcast_to(mine[None], (count,) + mine.shape)
    full = lax.all_to_all(send, axis, 0, 0, tiled=True)
    return full.reshape(rows, block.shape[1])


def spread(block, axis, source, pair_axis):
    core = lax.axis_index(pair_axis) % 2
    half = block.shape[0] // 2
    mine = lax.dynamic_slice_in_dim(block, core * half, half, 0)
    got = scatter_gather(mine, axis, source)
    pairs = [(i, i ^ 1) for i in range(lax.axis_size(pair_axis))]
    other = lax.ppermute(got, pair_axis, pairs)
    low = jnp.where(core == 0, got, other)
    high = jnp.where(core == 0, other, got)
    return jnp.concatenate([low, high], axis=0)


def padded_2(block, sides, width):
    for axis, dim in sides:
        count = lax.axis_size(axis)
        forward = [(i, i + 1) for i in range(count - 1)]
        backward = [(target, source) for source, target in forward]
        low = lax.ppermute(
            lax.slice_in_dim(block, block.shape[dim] - width, None, axis=dim), axis, forward
        )
        high = lax.ppermute(lax.slice_in_dim(block, 0, width, axis=dim), axis, backward)
        block = jnp.concatenate([low, block, high], axis=dim)
    return block


def padded_last(block, axis, width):
    count = lax.axis_size(axis)
    forward = [(i, i + 1) for i in range(count - 1)]
    backward = [(target, source) for source, target in forward]
    lead, rows = block.shape[0], block.shape[1]

    def pack(strip):
        return jnp.swapaxes(strip, 1, 2).reshape(lead * width, rows)

    def unpack(flat):
        return jnp.swapaxes(flat.reshape(lead, width, rows), 1, 2)

    low = unpack(lax.ppermute(pack(block[:, :, block.shape[2] - width :]), axis, forward))
    high = unpack(lax.ppermute(pack(block[:, :, :width]), axis, backward))
    return jnp.concatenate([low, block, high], axis=2)


def sweeps_kernel(rows_ref, coupling_ref, loading_ref, stiff_ref, side_ref, out_ref, picked_ref, load_scr, motion_ref, next_ref):
    fields = out_ref.shape[0]
    ext_rows, cells = loading_ref.shape[1], loading_ref.shape[2]
    rows, cols = load_scr.shape[1], load_scr.shape[2]
    width = SWEEPS - 1
    load_scr[:, ext_rows:, :] = jnp.zeros((fields + 1, rows - ext_rows, cols), jnp.float32)
    for a in range(fields):
        load_scr[a, :ext_rows, :cells] = loading_ref[a]
    load_scr[fields, :ext_rows, :cells] = stiff_ref[...]
    load_scr[:, :ext_rows, cells:] = side_ref[...]
    stiffness = load_scr[fields]
    for a in range(fields):
        diagonal = 4.0 * stiffness + coupling_ref[a, a]
        motion_ref[a] = chebyshev_weight(0) * (load_scr[a] / diagonal)
    source, target = motion_ref, next_ref
    for sweep in range(1, SWEEPS):
        for a in range(fields):
            centre = source[a]
            beside = (
                pltpu.roll(centre, rows - 1, 0)
                + pltpu.roll(centre, 1, 0)
                + pltpu.roll(centre, cols - 1, 1)
                + pltpu.roll(centre, 1, 1)
            )
            mixing = coupling_ref[a, 0] * source[0]
            for b in range(1, fields):
                mixing = mixing + coupling_ref[a, b] * source[b]
            applied = stiffness * (4.0 * centre - beside) + mixing
            diagonal = 4.0 * stiffness + coupling_ref[a, a]
            target[a] = centre + chebyshev_weight(sweep) * ((load_scr[a] - applied) / diagonal)
        source, target = target, source
    out_rows = out_ref.shape[1]
    for a in range(fields):
        out_ref[a] = pltpu.roll(source[a], rows - width, 0)[:out_rows, :cells]
    for slot in range(picked_ref.shape[1]):
        row = rows_ref[slot] + width
        for a in range(fields):
            picked_ref[a, pl.ds(slot, 1), :] = source[a, pl.ds(row, 1), pl.ds(0, cells)]


def run_sweeps(slot_row, coupling, loading, stiffness, side, out_rows):
    fields, ext_rows, cells = loading.shape
    rows = -(-ext_rows // 8) * 8
    cols = cells + side.shape[2]
    smem = pl.BlockSpec(memory_space=pltpu.SMEM)
    vmem = pl.BlockSpec(memory_space=pltpu.VMEM)
    return pl.pallas_call(
        sweeps_kernel,
        out_shape=(
            jax.ShapeDtypeStruct((fields, out_rows, cells), jnp.float32),
            jax.ShapeDtypeStruct((fields, slot_row.shape[0], cells), jnp.float32),
        ),
        in_specs=[smem, smem, vmem, vmem, vmem],
        out_specs=(vmem, vmem),
        scratch_shapes=[
            pltpu.VMEM((fields + 1, rows, cols), jnp.float32),
            pltpu.VMEM((fields, rows, cols), jnp.float32),
            pltpu.VMEM((fields, rows, cols), jnp.float32),
        ],
    )(slot_row, coupling, loading, stiffness, side)


def girth_side(blocks, axis, width, lanes):
    count = lax.axis_size(axis)
    forward = [(i, i + 1) for i in range(count - 1)]
    backward = [(target, source) for source, target in forward]
    lead = sum(block.shape[0] for block in blocks)
    rows = blocks[0].shape[1]
    size = blocks[0].shape[2]

    def pack(start):
        strip = jnp.concatenate([block[:, :, start : start + width] for block in blocks], axis=0)
        return jnp.swapaxes(strip, 1, 2).reshape(lead * width, rows)

    def unpack(flat):
        return jnp.swapaxes(flat.reshape(lead, width, rows), 1, 2)

    before = unpack(lax.ppermute(pack(size - width), axis, forward))
    after = unpack(lax.ppermute(pack(0), axis, backward))
    gap = jnp.zeros((lead, rows, lanes - 2 * width), before.dtype)
    return jnp.concatenate([after, gap, before], axis=2)


def chebyshev_weight(sweep):
    return 1.0 / (1.0 + 0.9 * math.cos(math.pi * (2 * sweep + 1) / (2 * SWEEPS)))


def operate_padded(padded, stiffness, coupling):
    centre = padded[:, 1:-1, 1:-1]
    beside = padded[:, 2:, 1:-1] + padded[:, :-2, 1:-1] + padded[:, 1:-1, 2:] + padded[:, 1:-1, :-2]
    mixing = jnp.einsum("ab,bij->aij", coupling, centre, precision=lax.Precision.HIGHEST)
    return stiffness * (4.0 * centre - beside) + mixing


def square_pairs(values, axis_at):
    first = jnp.take(values, 0, axis=axis_at)
    second = jnp.take(values, 1, axis=axis_at)
    third = jnp.take(values, 2, axis=axis_at)
    fourth = jnp.take(values, 3, axis=axis_at)
    return jnp.stack(
        [first * first + second * second, third * third + fourth * fourth], axis=axis_at
    )


def on_device(
    wave_amplitude,
    load_bank,
    freq_owner,
    thickness_class,
    class_stiffness,
    coupling,
    stress_map,
    psd_weight,
    hotspot_tile,
    hotspot_owner,
    prior_moments,
):
    row_count = wave_amplitude.shape[1]
    girth_cells = load_bank.shape[1]
    mode_count = load_bank.shape[0]
    width = SWEEPS - 1
    root = freq_owner[0]
    stiffness = jnp.zeros((row_count, girth_cells), jnp.float32)
    for level in range(class_stiffness.shape[0]):
        stiffness = stiffness + jnp.where(thickness_class == level, class_stiffness[level], 0.0)
    amplitude_ext = padded_2(wave_amplitude, (("length", 1),), width)
    stiffness_rows = padded_2(stiffness, (("length", 0),), width)
    factors = spread(load_bank, "girth", root, "length")
    ext_rows = row_count + 2 * width
    loading = jnp.dot(amplitude_ext.reshape(6 * ext_rows, mode_count), factors, preferred_element_type=jnp.float32)
    loading = loading.reshape(6, ext_rows, girth_cells)
    girth_count = lax.axis_size("girth")
    tile_ids = hotspot_tile[0]
    owner_ids = hotspot_owner[0, :, 0]
    listed = owner_ids.shape[0]
    positions = jnp.arange(listed, dtype=jnp.int32)
    matching = owner_ids[:, None] == owner_ids[None, :]
    earlier = positions[None, :] < positions[:, None]
    slot_rank = jnp.sum(jnp.logical_and(matching, earlier).astype(jnp.int32), axis=1)
    target = owner_ids * CAP + slot_rank
    slots = jnp.arange(girth_count * CAP, dtype=jnp.int32)
    hit = target[None, :] == slots[:, None]
    filled = jnp.any(hit, axis=1)
    slot_row = jnp.sum(jnp.where(hit, tile_ids[None, :], 0), axis=1)
    stiffness_at = jnp.take(stiffness, slot_row, axis=0)
    side = girth_side([loading, stiffness_rows[None]], "girth", width, 128)
    motion, motion_at = run_sweeps(slot_row, coupling, loading, stiffness_rows, side, row_count)
    stress_rows = stiffness_at[:, None, :] * jnp.einsum(
        "ka,aij->ikj", stress_map, motion_at, precision=lax.Precision.HIGHEST
    )
    spectra = square_pairs(stress_rows, 1)
    outbox = jnp.where(filled[:, None, None], spectra, 0.0)
    outbox = outbox.reshape(girth_count, CAP * 2 * girth_cells // 128, 128)
    received = lax.all_to_all(outbox, "girth", split_axis=0, concat_axis=0, tiled=True)
    received = received.reshape(girth_count, CAP, 2, girth_cells)
    hotspot_moments = prior_moments + (psd_weight[0] * received)[None, None]
    return (motion, hotspot_moments)


def solution(mesh):
    return jax.shard_map(
        on_device,
        mesh=mesh,
        in_specs=(
            P(None, "length", "girth"),
            P("girth", None),
            P(),
            P("length", "girth"),
            P(),
            P(),
            P(),
            P(),
            P("length", "girth"),
            P("length", "girth", None),
            P("length", "girth", None, None, None, None),
        ),
        out_specs=(P(None, "length", "girth"), P("length", "girth", None, None, None, None)),
        check_vma=False,
    )
```

```python
import math

import jax
import jax.numpy as jnp
from jax import lax
from jax.sharding import PartitionSpec as P
from jax.experimental import pallas as pl
from jax.experimental.pallas import tpu as pltpu

SWEEPS = 4
CAP = 2


def scatter_gather(block, axis, source):
    count = lax.axis_size(axis)
    rows = block.shape[0]
    send = block.reshape(count, rows // count, block.shape[1])
    got = lax.all_to_all(send, axis, 0, 0, tiled=True)
    mine = lax.dynamic_index_in_dim(got, source, 0, keepdims=False)
    send = jnp.broadcast_to(mine[None], (count,) + mine.shape)
    full = lax.all_to_all(send, axis, 0, 0, tiled=True)
    return full.reshape(rows, block.shape[1])


def spread_product(amplitude, block, axis, source, pair_axis):
    core = lax.axis_index(pair_axis) % 2
    half = block.shape[0] // 2
    mine = lax.dynamic_slice_in_dim(block, core * half, half, 0)
    got = scatter_gather(mine, axis, source)
    pairs = [(i, i ^ 1) for i in range(lax.axis_size(pair_axis))]
    other = lax.ppermute(got, pair_axis, pairs)
    low, high = amplitude[:, :half], amplitude[:, half:]
    own_part = jnp.dot(jnp.where(core == 0, low, high), got, preferred_element_type=jnp.float32)
    own_part, other = lax.optimization_barrier((own_part, other))
    other_part = jnp.dot(jnp.where(core == 0, high, low), other, preferred_element_type=jnp.float32)
    return own_part + other_part


def padded_2(block, sides, width):
    for axis, dim in sides:
        count = lax.axis_size(axis)
        forward = [(i, i + 1) for i in range(count - 1)]
        backward = [(target, source) for source, target in forward]
        low = lax.ppermute(
            lax.slice_in_dim(block, block.shape[dim] - width, None, axis=dim), axis, forward
        )
        high = lax.ppermute(lax.slice_in_dim(block, 0, width, axis=dim), axis, backward)
        block = jnp.concatenate([low, block, high], axis=dim)
    return block


def padded_last(block, axis, width):
    count = lax.axis_size(axis)
    forward = [(i, i + 1) for i in range(count - 1)]
    backward = [(target, source) for source, target in forward]
    lead, rows = block.shape[0], block.shape[1]

    def pack(strip):
        return jnp.swapaxes(strip, 1, 2).reshape(lead * width, rows)

    def unpack(flat):
        return jnp.swapaxes(flat.reshape(lead, width, rows), 1, 2)

    low = unpack(lax.ppermute(pack(block[:, :, block.shape[2] - width :]), axis, forward))
    high = unpack(lax.ppermute(pack(block[:, :, :width]), axis, backward))
    return jnp.concatenate([low, block, high], axis=2)


def sweeps_kernel(rows_ref, coupling_ref, loading_ref, stiff_ref, side_ref, out_ref, picked_ref, load_scr, motion_ref, next_ref):
    fields = out_ref.shape[0]
    ext_rows, cells = loading_ref.shape[1], loading_ref.shape[2]
    rows, cols = load_scr.shape[1], load_scr.shape[2]
    width = SWEEPS - 1
    load_scr[:, ext_rows:, :] = jnp.zeros((fields + 1, rows - ext_rows, cols), jnp.float32)
    for a in range(fields):
        load_scr[a, :ext_rows, :cells] = loading_ref[a]
    load_scr[fields, :ext_rows, :cells] = stiff_ref[...]
    load_scr[:, :ext_rows, cells:] = side_ref[...]
    stiffness = load_scr[fields]
    for a in range(fields):
        diagonal = 4.0 * stiffness + coupling_ref[a, a]
        motion_ref[a] = chebyshev_weight(0) * (load_scr[a] / diagonal)
    source, target = motion_ref, next_ref
    for sweep in range(1, SWEEPS):
        for a in range(fields):
            centre = source[a]
            beside = (
                pltpu.roll(centre, rows - 1, 0)
                + pltpu.roll(centre, 1, 0)
                + pltpu.roll(centre, cols - 1, 1)
                + pltpu.roll(centre, 1, 1)
            )
            mixing = coupling_ref[a, 0] * source[0]
            for b in range(1, fields):
                mixing = mixing + coupling_ref[a, b] * source[b]
            applied = stiffness * (4.0 * centre - beside) + mixing
            diagonal = 4.0 * stiffness + coupling_ref[a, a]
            target[a] = centre + chebyshev_weight(sweep) * ((load_scr[a] - applied) / diagonal)
        source, target = target, source
    out_rows = out_ref.shape[1]
    for a in range(fields):
        out_ref[a] = pltpu.roll(source[a], rows - width, 0)[:out_rows, :cells]
    for slot in range(picked_ref.shape[1]):
        row = rows_ref[slot] + width
        for a in range(fields):
            picked_ref[a, pl.ds(slot, 1), :] = source[a, pl.ds(row, 1), pl.ds(0, cells)]


def run_sweeps(slot_row, coupling, loading, stiffness, side, out_rows):
    fields, ext_rows, cells = loading.shape
    rows = -(-ext_rows // 8) * 8
    cols = cells + side.shape[2]
    smem = pl.BlockSpec(memory_space=pltpu.SMEM)
    vmem = pl.BlockSpec(memory_space=pltpu.VMEM)
    return pl.pallas_call(
        sweeps_kernel,
        out_shape=(
            jax.ShapeDtypeStruct((fields, out_rows, cells), jnp.float32),
            jax.ShapeDtypeStruct((fields, slot_row.shape[0], cells), jnp.float32),
        ),
        in_specs=[smem, smem, vmem, vmem, vmem],
        out_specs=(vmem, vmem),
        scratch_shapes=[
            pltpu.VMEM((fields + 1, rows, cols), jnp.float32),
            pltpu.VMEM((fields, rows, cols), jnp.float32),
            pltpu.VMEM((fields, rows, cols), jnp.float32),
        ],
    )(slot_row, coupling, loading, stiffness, side)


def girth_side(blocks, axis, width, lanes):
    count = lax.axis_size(axis)
    forward = [(i, i + 1) for i in range(count - 1)]
    backward = [(target, source) for source, target in forward]
    lead = sum(block.shape[0] for block in blocks)
    rows = blocks[0].shape[1]
    size = blocks[0].shape[2]

    def pack(start):
        strip = jnp.concatenate([block[:, :, start : start + width] for block in blocks], axis=0)
        return jnp.swapaxes(strip, 1, 2).reshape(lead * width, rows)

    def unpack(flat):
        return jnp.swapaxes(flat.reshape(lead, width, rows), 1, 2)

    before = unpack(lax.ppermute(pack(size - width), axis, forward))
    after = unpack(lax.ppermute(pack(0), axis, backward))
    gap = jnp.zeros((lead, rows, lanes - 2 * width), before.dtype)
    return jnp.concatenate([after, gap, before], axis=2)


def chebyshev_weight(sweep):
    return 1.0 / (1.0 + 0.9 * math.cos(math.pi * (2 * sweep + 1) / (2 * SWEEPS)))


def operate_padded(padded, stiffness, coupling):
    centre = padded[:, 1:-1, 1:-1]
    beside = padded[:, 2:, 1:-1] + padded[:, :-2, 1:-1] + padded[:, 1:-1, 2:] + padded[:, 1:-1, :-2]
    mixing = jnp.einsum("ab,bij->aij", coupling, centre, precision=lax.Precision.HIGHEST)
    return stiffness * (4.0 * centre - beside) + mixing


def square_pairs(values, axis_at):
    first = jnp.take(values, 0, axis=axis_at)
    second = jnp.take(values, 1, axis=axis_at)
    third = jnp.take(values, 2, axis=axis_at)
    fourth = jnp.take(values, 3, axis=axis_at)
    return jnp.stack(
        [first * first + second * second, third * third + fourth * fourth], axis=axis_at
    )


def on_device(
    wave_amplitude,
    load_bank,
    freq_owner,
    thickness_class,
    class_stiffness,
    coupling,
    stress_map,
    psd_weight,
    hotspot_tile,
    hotspot_owner,
    prior_moments,
):
    row_count = wave_amplitude.shape[1]
    girth_cells = load_bank.shape[1]
    mode_count = load_bank.shape[0]
    width = SWEEPS - 1
    root = freq_owner[0]
    stiffness = jnp.zeros((row_count, girth_cells), jnp.float32)
    for level in range(class_stiffness.shape[0]):
        stiffness = stiffness + jnp.where(thickness_class == level, class_stiffness[level], 0.0)
    amplitude_ext = padded_2(wave_amplitude, (("length", 1),), width)
    stiffness_rows = padded_2(stiffness, (("length", 0),), width)
    ext_rows = row_count + 2 * width
    loading = spread_product(amplitude_ext.reshape(6 * ext_rows, mode_count), load_bank, "girth", root, "length")
    loading = loading.reshape(6, ext_rows, girth_cells)
    girth_count = lax.axis_size("girth")
    tile_ids = hotspot_tile[0]
    owner_ids = hotspot_owner[0, :, 0]
    listed = owner_ids.shape[0]
    positions = jnp.arange(listed, dtype=jnp.int32)
    matching = owner_ids[:, None] == owner_ids[None, :]
    earlier = positions[None, :] < positions[:, None]
    slot_rank = jnp.sum(jnp.logical_and(matching, earlier).astype(jnp.int32), axis=1)
    target = owner_ids * CAP + slot_rank
    slots = jnp.arange(girth_count * CAP, dtype=jnp.int32)
    hit = target[None, :] == slots[:, None]
    filled = jnp.any(hit, axis=1)
    slot_row = jnp.sum(jnp.where(hit, tile_ids[None, :], 0), axis=1)
    stiffness_at = jnp.take(stiffness, slot_row, axis=0)
    side = girth_side([loading, stiffness_rows[None]], "girth", width, 128)
    motion, motion_at = run_sweeps(slot_row, coupling, loading, stiffness_rows, side, row_count)
    stress_rows = stiffness_at[:, None, :] * jnp.einsum(
        "ka,aij->ikj", stress_map, motion_at, precision=lax.Precision.HIGHEST
    )
    spectra = square_pairs(stress_rows, 1)
    outbox = jnp.where(filled[:, None, None], spectra, 0.0)
    outbox = outbox.reshape(girth_count, CAP * 2 * girth_cells // 128, 128)
    received = lax.all_to_all(outbox, "girth", split_axis=0, concat_axis=0, tiled=True)
    received = received.reshape(girth_count, CAP, 2, girth_cells)
    hotspot_moments = prior_moments + (psd_weight[0] * received)[None, None]
    return (motion, hotspot_moments)


def solution(mesh):
    return jax.shard_map(
        on_device,
        mesh=mesh,
        in_specs=(
            P(None, "length", "girth"),
            P("girth", None),
            P(),
            P("length", "girth"),
            P(),
            P(),
            P(),
            P(),
            P("length", "girth"),
            P("length", "girth", None),
            P("length", "girth", None, None, None, None),
        ),
        out_specs=(P(None, "length", "girth"), P("length", "girth", None, None, None, None)),
        check_vma=False,
    )
```

```python
import math

import jax
import jax.numpy as jnp
from jax import lax
from jax.sharding import PartitionSpec as P
from jax.experimental import pallas as pl
from jax.experimental.pallas import tpu as pltpu

SWEEPS = 4
CAP = 2


def scatter_gather(block, axis, source):
    count = lax.axis_size(axis)
    rows = block.shape[0]
    send = block.reshape(count, rows // count, block.shape[1])
    got = lax.all_to_all(send, axis, 0, 0, tiled=True)
    mine = lax.dynamic_index_in_dim(got, source, 0, keepdims=False)
    send = jnp.broadcast_to(mine[None], (count,) + mine.shape)
    full = lax.all_to_all(send, axis, 0, 0, tiled=True)
    return full.reshape(rows, block.shape[1])


def spread(block, axis, source, pair_axis):
    core = lax.axis_index(pair_axis) % 2
    half = block.shape[0] // 2
    mine = lax.dynamic_slice_in_dim(block, core * half, half, 0)
    got = scatter_gather(mine, axis, source)
    pairs = [(i, i ^ 1) for i in range(lax.axis_size(pair_axis))]
    other = lax.ppermute(got, pair_axis, pairs)
    low = jnp.where(core == 0, got, other)
    high = jnp.where(core == 0, other, got)
    return jnp.concatenate([low, high], axis=0)


def padded_2(block, sides, width):
    for axis, dim in sides:
        count = lax.axis_size(axis)
        forward = [(i, i + 1) for i in range(count - 1)]
        backward = [(target, source) for source, target in forward]
        low = lax.ppermute(
            lax.slice_in_dim(block, block.shape[dim] - width, None, axis=dim), axis, forward
        )
        high = lax.ppermute(lax.slice_in_dim(block, 0, width, axis=dim), axis, backward)
        block = jnp.concatenate([low, block, high], axis=dim)
    return block


def padded_last(block, axis, width):
    count = lax.axis_size(axis)
    forward = [(i, i + 1) for i in range(count - 1)]
    backward = [(target, source) for source, target in forward]
    lead, rows = block.shape[0], block.shape[1]

    def pack(strip):
        return jnp.swapaxes(strip, 1, 2).reshape(lead * width, rows)

    def unpack(flat):
        return jnp.swapaxes(flat.reshape(lead, width, rows), 1, 2)

    low = unpack(lax.ppermute(pack(block[:, :, block.shape[2] - width :]), axis, forward))
    high = unpack(lax.ppermute(pack(block[:, :, :width]), axis, backward))
    return jnp.concatenate([low, block, high], axis=2)


def sweeps_kernel(
    rows_ref, filled_ref, coupling_ref, stress_ref, loading_ref, stiff_ref, side_ref,
    out_ref, outbox_ref, load_scr, motion_ref, next_ref,
):
    fields = out_ref.shape[0]
    ext_rows, cells = loading_ref.shape[1], loading_ref.shape[2]
    rows, cols = load_scr.shape[1], load_scr.shape[2]
    width = SWEEPS - 1
    load_scr[:, ext_rows:, :] = jnp.zeros((fields + 1, rows - ext_rows, cols), jnp.float32)
    for a in range(fields):
        load_scr[a, :ext_rows, :cells] = loading_ref[a]
    load_scr[fields, :ext_rows, :cells] = stiff_ref[...]
    load_scr[:, :ext_rows, cells:] = side_ref[...]
    stiffness = load_scr[fields]
    for a in range(fields):
        diagonal = 4.0 * stiffness + coupling_ref[a, a]
        motion_ref[a] = chebyshev_weight(0) * (load_scr[a] / diagonal)
    source, target = motion_ref, next_ref
    for sweep in range(1, SWEEPS):
        for a in range(fields):
            centre = source[a]
            beside = (
                pltpu.roll(centre, rows - 1, 0)
                + pltpu.roll(centre, 1, 0)
                + pltpu.roll(centre, cols - 1, 1)
                + pltpu.roll(centre, 1, 1)
            )
            mixing = coupling_ref[a, 0] * source[0]
            for b in range(1, fields):
                mixing = mixing + coupling_ref[a, b] * source[b]
            applied = stiffness * (4.0 * centre - beside) + mixing
            diagonal = 4.0 * stiffness + coupling_ref[a, a]
            target[a] = centre + chebyshev_weight(sweep) * ((load_scr[a] - applied) / diagonal)
        source, target = target, source
    out_rows = out_ref.shape[1]
    for a in range(fields):
        out_ref[a] = pltpu.roll(source[a], rows - width, 0)[:out_rows, :cells]
    per_owner = outbox_ref.shape[1] // (2 * CAP)
    for slot in range(rows_ref.shape[0]):
        row = rows_ref[slot] + width
        lines = [source[a, pl.ds(row, 1), pl.ds(0, cells)] for a in range(fields)]
        stiff_line = load_scr[fields, pl.ds(row, 1), pl.ds(0, cells)]
        stress = []
        for k in range(stress_ref.shape[0]):
            mapped = stress_ref[k, 0] * lines[0]
            for a in range(1, fields):
                mapped = mapped + stress_ref[k, a] * lines[a]
            stress.append(stiff_line * mapped)
        keep = filled_ref[slot] != 0
        for d in range(2):
            spectrum = stress[2 * d] * stress[2 * d] + stress[2 * d + 1] * stress[2 * d + 1]
            spectrum = jnp.where(keep, spectrum, 0.0)
            for h in range(per_owner):
                place = ((slot % CAP) * 2 + d) * per_owner + h
                outbox_ref[slot // CAP, pl.ds(place, 1), :] = spectrum[:, h * 128 : (h + 1) * 128]


def run_sweeps(slot_row, filled, coupling, stress_map, loading, stiffness, side, out_rows):
    fields, ext_rows, cells = loading.shape
    rows = -(-ext_rows // 8) * 8
    cols = cells + side.shape[2]
    smem = pl.BlockSpec(memory_space=pltpu.SMEM)
    vmem = pl.BlockSpec(memory_space=pltpu.VMEM)
    return pl.pallas_call(
        sweeps_kernel,
        out_shape=(
            jax.ShapeDtypeStruct((fields, out_rows, cells), jnp.float32),
            jax.ShapeDtypeStruct((slot_row.shape[0] // CAP, CAP * 2 * cells // 128, 128), jnp.float32),
        ),
        in_specs=[smem, smem, smem, smem, vmem, vmem, vmem],
        out_specs=(vmem, vmem),
        scratch_shapes=[
            pltpu.VMEM((fields + 1, rows, cols), jnp.float32),
            pltpu.VMEM((fields, rows, cols), jnp.float32),
            pltpu.VMEM((fields, rows, cols), jnp.float32),
        ],
    )(slot_row, filled, coupling, stress_map, loading, stiffness, side)


def girth_side(blocks, axis, width, lanes):
    count = lax.axis_size(axis)
    forward = [(i, i + 1) for i in range(count - 1)]
    backward = [(target, source) for source, target in forward]
    lead = sum(block.shape[0] for block in blocks)
    rows = blocks[0].shape[1]
    size = blocks[0].shape[2]

    def pack(start):
        strip = jnp.concatenate([block[:, :, start : start + width] for block in blocks], axis=0)
        return jnp.swapaxes(strip, 1, 2).reshape(lead * width, rows)

    def unpack(flat):
        return jnp.swapaxes(flat.reshape(lead, width, rows), 1, 2)

    before = unpack(lax.ppermute(pack(size - width), axis, forward))
    after = unpack(lax.ppermute(pack(0), axis, backward))
    gap = jnp.zeros((lead, rows, lanes - 2 * width), before.dtype)
    return jnp.concatenate([after, gap, before], axis=2)


def chebyshev_weight(sweep):
    return 1.0 / (1.0 + 0.9 * math.cos(math.pi * (2 * sweep + 1) / (2 * SWEEPS)))


def operate_padded(padded, stiffness, coupling):
    centre = padded[:, 1:-1, 1:-1]
    beside = padded[:, 2:, 1:-1] + padded[:, :-2, 1:-1] + padded[:, 1:-1, 2:] + padded[:, 1:-1, :-2]
    mixing = jnp.einsum("ab,bij->aij", coupling, centre, precision=lax.Precision.HIGHEST)
    return stiffness * (4.0 * centre - beside) + mixing


def square_pairs(values, axis_at):
    first = jnp.take(values, 0, axis=axis_at)
    second = jnp.take(values, 1, axis=axis_at)
    third = jnp.take(values, 2, axis=axis_at)
    fourth = jnp.take(values, 3, axis=axis_at)
    return jnp.stack(
        [first * first + second * second, third * third + fourth * fourth], axis=axis_at
    )


def on_device(
    wave_amplitude,
    load_bank,
    freq_owner,
    thickness_class,
    class_stiffness,
    coupling,
    stress_map,
    psd_weight,
    hotspot_tile,
    hotspot_owner,
    prior_moments,
):
    row_count = wave_amplitude.shape[1]
    girth_cells = load_bank.shape[1]
    mode_count = load_bank.shape[0]
    width = SWEEPS - 1
    root = freq_owner[0]
    stiffness = jnp.zeros((row_count, girth_cells), jnp.float32)
    for level in range(class_stiffness.shape[0]):
        stiffness = stiffness + jnp.where(thickness_class == level, class_stiffness[level], 0.0)
    amplitude_ext = padded_2(wave_amplitude, (("length", 1),), width)
    stiffness_rows = padded_2(stiffness, (("length", 0),), width)
    factors = spread(load_bank, "girth", root, "length")
    ext_rows = row_count + 2 * width
    loading = jnp.dot(amplitude_ext.reshape(6 * ext_rows, mode_count), factors, preferred_element_type=jnp.float32)
    loading = loading.reshape(6, ext_rows, girth_cells)
    girth_count = lax.axis_size("girth")
    tile_ids = hotspot_tile[0]
    owner_ids = hotspot_owner[0, :, 0]
    listed = owner_ids.shape[0]
    positions = jnp.arange(listed, dtype=jnp.int32)
    matching = owner_ids[:, None] == owner_ids[None, :]
    earlier = positions[None, :] < positions[:, None]
    slot_rank = jnp.sum(jnp.logical_and(matching, earlier).astype(jnp.int32), axis=1)
    target = owner_ids * CAP + slot_rank
    slots = jnp.arange(girth_count * CAP, dtype=jnp.int32)
    hit = target[None, :] == slots[:, None]
    filled = jnp.any(hit, axis=1)
    slot_row = jnp.sum(jnp.where(hit, tile_ids[None, :], 0), axis=1)
    side = girth_side([loading, stiffness_rows[None]], "girth", width, 128)
    motion, outbox = run_sweeps(
        slot_row, filled.astype(jnp.int32), coupling, stress_map, loading, stiffness_rows, side, row_count
    )
    received = lax.all_to_all(outbox, "girth", split_axis=0, concat_axis=0, tiled=True)
    received = received.reshape(girth_count, CAP, 2, girth_cells)
    hotspot_moments = prior_moments + (psd_weight[0] * received)[None, None]
    return (motion, hotspot_moments)


def solution(mesh):
    return jax.shard_map(
        on_device,
        mesh=mesh,
        in_specs=(
            P(None, "length", "girth"),
            P("girth", None),
            P(),
            P("length", "girth"),
            P(),
            P(),
            P(),
            P(),
            P("length", "girth"),
            P("length", "girth", None),
            P("length", "girth", None, None, None, None),
        ),
        out_specs=(P(None, "length", "girth"), P("length", "girth", None, None, None, None)),
        check_vma=False,
    )
```

```python
import math

import jax
import jax.numpy as jnp
from jax import lax
from jax.sharding import PartitionSpec as P
from jax.experimental import pallas as pl
from jax.experimental.pallas import tpu as pltpu

SWEEPS = 4
CAP = 2


def scatter_gather(block, axis, source):
    count = lax.axis_size(axis)
    rows = block.shape[0]
    send = block.reshape(count, rows // count, block.shape[1])
    got = lax.all_to_all(send, axis, 0, 0, tiled=True)
    mine = lax.dynamic_index_in_dim(got, source, 0, keepdims=False)
    send = jnp.broadcast_to(mine[None], (count,) + mine.shape)
    full = lax.all_to_all(send, axis, 0, 0, tiled=True)
    return full.reshape(rows, block.shape[1])


def spread(block, axis, source, pair_axis):
    core = lax.axis_index(pair_axis) % 2
    half = block.shape[0] // 2
    mine = lax.dynamic_slice_in_dim(block, core * half, half, 0)
    got = scatter_gather(mine, axis, source)
    pairs = [(i, i ^ 1) for i in range(lax.axis_size(pair_axis))]
    other = lax.ppermute(got, pair_axis, pairs)
    low = jnp.where(core == 0, got, other)
    high = jnp.where(core == 0, other, got)
    return jnp.concatenate([low, high], axis=0)


def padded_2(block, sides, width):
    for axis, dim in sides:
        count = lax.axis_size(axis)
        forward = [(i, i + 1) for i in range(count - 1)]
        backward = [(target, source) for source, target in forward]
        low = lax.ppermute(
            lax.slice_in_dim(block, block.shape[dim] - width, None, axis=dim), axis, forward
        )
        high = lax.ppermute(lax.slice_in_dim(block, 0, width, axis=dim), axis, backward)
        block = jnp.concatenate([low, block, high], axis=dim)
    return block


def padded_last(block, axis, width):
    count = lax.axis_size(axis)
    forward = [(i, i + 1) for i in range(count - 1)]
    backward = [(target, source) for source, target in forward]
    lead, rows = block.shape[0], block.shape[1]

    def pack(strip):
        return jnp.swapaxes(strip, 1, 2).reshape(lead * width, rows)

    def unpack(flat):
        return jnp.swapaxes(flat.reshape(lead, width, rows), 1, 2)

    low = unpack(lax.ppermute(pack(block[:, :, block.shape[2] - width :]), axis, forward))
    high = unpack(lax.ppermute(pack(block[:, :, :width]), axis, backward))
    return jnp.concatenate([low, block, high], axis=2)


def sweeps_kernel(rows_ref, coupling_ref, loading_ref, stiff_ref, side_ref, out_ref, picked_ref, load_scr, motion_ref, next_ref):
    fields = out_ref.shape[0]
    ext_rows, cells = loading_ref.shape[1], loading_ref.shape[2]
    rows, cols = load_scr.shape[1], load_scr.shape[2]
    width = SWEEPS - 1
    load_scr[:, ext_rows:, :] = jnp.zeros((fields + 1, rows - ext_rows, cols), jnp.float32)
    for a in range(fields):
        load_scr[a, :ext_rows, :cells] = loading_ref[a]
    load_scr[fields, :ext_rows, :cells] = stiff_ref[...]
    load_scr[:, :ext_rows, cells:] = side_ref[...]
    stiffness = load_scr[fields]
    for a in range(fields):
        diagonal = 4.0 * stiffness + coupling_ref[a, a]
        motion_ref[a] = chebyshev_weight(0) * (load_scr[a] / diagonal)
    source, target = motion_ref, next_ref
    for sweep in range(1, SWEEPS):
        for a in range(fields):
            centre = source[a]
            beside = (
                pltpu.roll(centre, rows - 1, 0)
                + pltpu.roll(centre, 1, 0)
                + pltpu.roll(centre, cols - 1, 1)
                + pltpu.roll(centre, 1, 1)
            )
            mixing = coupling_ref[a, 0] * source[0]
            for b in range(1, fields):
                mixing = mixing + coupling_ref[a, b] * source[b]
            applied = stiffness * (4.0 * centre - beside) + mixing
            diagonal = 4.0 * stiffness + coupling_ref[a, a]
            target[a] = centre + chebyshev_weight(sweep) * ((load_scr[a] - applied) / diagonal)
        source, target = target, source
    out_rows = out_ref.shape[1]
    for a in range(fields):
        out_ref[a] = pltpu.roll(source[a], rows - width, 0)[:out_rows, :cells]
    for slot in range(picked_ref.shape[1]):
        row = rows_ref[slot] + width
        for a in range(fields):
            picked_ref[a, pl.ds(slot, 1), :] = source[a, pl.ds(row, 1), pl.ds(0, cells)]


def run_sweeps(slot_row, coupling, loading, stiffness, side, out_rows):
    fields, ext_rows, cells = loading.shape
    rows = -(-ext_rows // 8) * 8
    cols = cells + side.shape[2]
    smem = pl.BlockSpec(memory_space=pltpu.SMEM)
    vmem = pl.BlockSpec(memory_space=pltpu.VMEM)
    return pl.pallas_call(
        sweeps_kernel,
        out_shape=(
            jax.ShapeDtypeStruct((fields, out_rows, cells), jnp.float32),
            jax.ShapeDtypeStruct((fields, slot_row.shape[0], cells), jnp.float32),
        ),
        in_specs=[smem, smem, vmem, vmem, vmem],
        out_specs=(vmem, vmem),
        scratch_shapes=[
            pltpu.VMEM((fields + 1, rows, cols), jnp.float32),
            pltpu.VMEM((fields, rows, cols), jnp.float32),
            pltpu.VMEM((fields, rows, cols), jnp.float32),
        ],
    )(slot_row, coupling, loading, stiffness, side)


def girth_side(blocks, axis, width, lanes):
    count = lax.axis_size(axis)
    forward = [(i, i + 1) for i in range(count - 1)]
    backward = [(target, source) for source, target in forward]
    lead = sum(block.shape[0] for block in blocks)
    rows = blocks[0].shape[1]
    size = blocks[0].shape[2]

    def pack(start):
        strip = jnp.concatenate([block[:, :, start : start + width] for block in blocks], axis=0)
        return jnp.swapaxes(strip, 1, 2).reshape(lead * width, rows)

    def unpack(flat):
        return jnp.swapaxes(flat.reshape(lead, width, rows), 1, 2)

    before = unpack(lax.ppermute(pack(size - width), axis, forward))
    after = unpack(lax.ppermute(pack(0), axis, backward))
    gap = jnp.zeros((lead, rows, lanes - 2 * width), before.dtype)
    return jnp.concatenate([after, gap, before], axis=2)


def chebyshev_weight(sweep):
    return 1.0 / (1.0 + 0.9 * math.cos(math.pi * (2 * sweep + 1) / (2 * SWEEPS)))


def operate_padded(padded, stiffness, coupling):
    centre = padded[:, 1:-1, 1:-1]
    beside = padded[:, 2:, 1:-1] + padded[:, :-2, 1:-1] + padded[:, 1:-1, 2:] + padded[:, 1:-1, :-2]
    mixing = jnp.einsum("ab,bij->aij", coupling, centre, precision=lax.Precision.HIGHEST)
    return stiffness * (4.0 * centre - beside) + mixing


def square_pairs(values, axis_at):
    first = jnp.take(values, 0, axis=axis_at)
    second = jnp.take(values, 1, axis=axis_at)
    third = jnp.take(values, 2, axis=axis_at)
    fourth = jnp.take(values, 3, axis=axis_at)
    return jnp.stack(
        [first * first + second * second, third * third + fourth * fourth], axis=axis_at
    )


def on_device(
    wave_amplitude,
    load_bank,
    freq_owner,
    thickness_class,
    class_stiffness,
    coupling,
    stress_map,
    psd_weight,
    hotspot_tile,
    hotspot_owner,
    prior_moments,
):
    row_count = wave_amplitude.shape[1]
    girth_cells = load_bank.shape[1]
    mode_count = load_bank.shape[0]
    width = SWEEPS - 1
    root = freq_owner[0]
    stiffness = jnp.zeros((row_count, girth_cells), jnp.float32)
    for level in range(class_stiffness.shape[0]):
        stiffness = stiffness + jnp.where(thickness_class == level, class_stiffness[level], 0.0)
    amplitude_ext = padded_2(wave_amplitude, (("length", 1),), width)
    stiffness_rows = padded_2(stiffness, (("length", 0),), width)
    factors = spread(load_bank, "girth", root, "length")
    ext_rows = row_count + 2 * width
    loading = jnp.dot(amplitude_ext.reshape(6 * ext_rows, mode_count), factors, preferred_element_type=jnp.float32)
    loading = loading.reshape(6, ext_rows, girth_cells)
    girth_count = lax.axis_size("girth")
    tile_ids = hotspot_tile[0]
    owner_ids = hotspot_owner[0, :, 0]
    listed = owner_ids.shape[0]
    positions = jnp.arange(listed, dtype=jnp.int32)
    matching = owner_ids[:, None] == owner_ids[None, :]
    earlier = positions[None, :] < positions[:, None]
    slot_rank = jnp.sum(jnp.logical_and(matching, earlier).astype(jnp.int32), axis=1)
    target = owner_ids * CAP + slot_rank
    slots = jnp.arange(girth_count * CAP, dtype=jnp.int32)
    hit = target[None, :] == slots[:, None]
    filled = jnp.any(hit, axis=1)
    slot_row = jnp.sum(jnp.where(hit, tile_ids[None, :], 0), axis=1)
    stiffness_at = jnp.take(stiffness, slot_row, axis=0)
    side = girth_side([loading, stiffness_rows[None]], "girth", width, 128)
    motion, motion_at = run_sweeps(slot_row, coupling, loading, stiffness_rows, side, row_count)
    stress = [
        stiffness_at * sum(stress_map[k, a] * motion_at[a] for a in range(motion_at.shape[0]))
        for k in range(stress_map.shape[0])
    ]
    spectra = jnp.stack(
        [stress[0] * stress[0] + stress[1] * stress[1], stress[2] * stress[2] + stress[3] * stress[3]], axis=1
    )
    outbox = jnp.where(filled[:, None, None], spectra, 0.0)
    outbox = outbox.reshape(girth_count, CAP * 2 * girth_cells // 128, 128)
    received = lax.all_to_all(outbox, "girth", split_axis=0, concat_axis=0, tiled=True)
    received = received.reshape(girth_count, CAP, 2, girth_cells)
    hotspot_moments = prior_moments + (psd_weight[0] * received)[None, None]
    return (motion, hotspot_moments)


def solution(mesh):
    return jax.shard_map(
        on_device,
        mesh=mesh,
        in_specs=(
            P(None, "length", "girth"),
            P("girth", None),
            P(),
            P("length", "girth"),
            P(),
            P(),
            P(),
            P(),
            P("length", "girth"),
            P("length", "girth", None),
            P("length", "girth", None, None, None, None),
        ),
        out_specs=(P(None, "length", "girth"), P("length", "girth", None, None, None, None)),
        check_vma=False,
    )
```

```python
import math

import jax
import jax.numpy as jnp
from jax import lax
from jax.sharding import PartitionSpec as P
from jax.experimental import pallas as pl
from jax.experimental.pallas import tpu as pltpu

SWEEPS = 4
CAP = 2


def scatter_gather(block, axis, source):
    count = lax.axis_size(axis)
    rows = block.shape[0]
    send = block.reshape(count, rows // count, block.shape[1])
    got = lax.all_to_all(send, axis, 0, 0, tiled=True)
    mine = lax.dynamic_index_in_dim(got, source, 0, keepdims=False)
    send = jnp.broadcast_to(mine[None], (count,) + mine.shape)
    full = lax.all_to_all(send, axis, 0, 0, tiled=True)
    return full.reshape(rows, block.shape[1])


def spread(block, axis, source, pair_axis):
    core = lax.axis_index(pair_axis) % 2
    half = block.shape[0] // 2
    mine = lax.dynamic_slice_in_dim(block, core * half, half, 0)
    got = scatter_gather(mine, axis, source)
    pairs = [(i, i ^ 1) for i in range(lax.axis_size(pair_axis))]
    other = lax.ppermute(got, pair_axis, pairs)
    low = jnp.where(core == 0, got, other)
    high = jnp.where(core == 0, other, got)
    return jnp.concatenate([low, high], axis=0)


def padded_2(block, sides, width):
    for axis, dim in sides:
        count = lax.axis_size(axis)
        forward = [(i, i + 1) for i in range(count - 1)]
        backward = [(target, source) for source, target in forward]
        low = lax.ppermute(
            lax.slice_in_dim(block, block.shape[dim] - width, None, axis=dim), axis, forward
        )
        high = lax.ppermute(lax.slice_in_dim(block, 0, width, axis=dim), axis, backward)
        block = jnp.concatenate([low, block, high], axis=dim)
    return block


def padded_last(block, axis, width):
    count = lax.axis_size(axis)
    forward = [(i, i + 1) for i in range(count - 1)]
    backward = [(target, source) for source, target in forward]
    lead, rows = block.shape[0], block.shape[1]

    def pack(strip):
        return jnp.swapaxes(strip, 1, 2).reshape(lead * width, rows)

    def unpack(flat):
        return jnp.swapaxes(flat.reshape(lead, width, rows), 1, 2)

    low = unpack(lax.ppermute(pack(block[:, :, block.shape[2] - width :]), axis, forward))
    high = unpack(lax.ppermute(pack(block[:, :, :width]), axis, backward))
    return jnp.concatenate([low, block, high], axis=2)


def sweeps_kernel(rows_ref, coupling_ref, loading_ref, stiff_ref, side_ref, out_ref, picked_ref, load_scr, motion_ref, next_ref):
    fields = out_ref.shape[0]
    ext_rows, cells = loading_ref.shape[1], loading_ref.shape[2]
    rows, cols = load_scr.shape[1], load_scr.shape[2]
    width = SWEEPS - 1
    load_scr[:, ext_rows:, :] = jnp.zeros((fields + 1, rows - ext_rows, cols), jnp.float32)
    for a in range(fields):
        load_scr[a, :ext_rows, :cells] = loading_ref[a]
    load_scr[fields, :ext_rows, :cells] = stiff_ref[...]
    load_scr[:, :ext_rows, cells:] = side_ref[...]
    stiffness = load_scr[fields]
    inverse = []
    for a in range(fields):
        inverse.append(1.0 / (4.0 * stiffness + coupling_ref[a, a]))
        motion_ref[a] = chebyshev_weight(0) * (load_scr[a] * inverse[a])
    source, target = motion_ref, next_ref
    for sweep in range(1, SWEEPS):
        for a in range(fields):
            centre = source[a]
            beside = (
                pltpu.roll(centre, rows - 1, 0)
                + pltpu.roll(centre, 1, 0)
                + pltpu.roll(centre, cols - 1, 1)
                + pltpu.roll(centre, 1, 1)
            )
            mixing = coupling_ref[a, 0] * source[0]
            for b in range(1, fields):
                mixing = mixing + coupling_ref[a, b] * source[b]
            applied = stiffness * (4.0 * centre - beside) + mixing
            target[a] = centre + chebyshev_weight(sweep) * ((load_scr[a] - applied) * inverse[a])
        source, target = target, source
    out_rows = out_ref.shape[1]
    for a in range(fields):
        out_ref[a] = pltpu.roll(source[a], rows - width, 0)[:out_rows, :cells]
    for slot in range(picked_ref.shape[1]):
        row = rows_ref[slot] + width
        for a in range(fields):
            picked_ref[a, pl.ds(slot, 1), :] = source[a, pl.ds(row, 1), pl.ds(0, cells)]


def run_sweeps(slot_row, coupling, loading, stiffness, side, out_rows):
    fields, ext_rows, cells = loading.shape
    rows = -(-ext_rows // 8) * 8
    cols = cells + side.shape[2]
    smem = pl.BlockSpec(memory_space=pltpu.SMEM)
    vmem = pl.BlockSpec(memory_space=pltpu.VMEM)
    return pl.pallas_call(
        sweeps_kernel,
        out_shape=(
            jax.ShapeDtypeStruct((fields, out_rows, cells), jnp.float32),
            jax.ShapeDtypeStruct((fields, slot_row.shape[0], cells), jnp.float32),
        ),
        in_specs=[smem, smem, vmem, vmem, vmem],
        out_specs=(vmem, vmem),
        scratch_shapes=[
            pltpu.VMEM((fields + 1, rows, cols), jnp.float32),
            pltpu.VMEM((fields, rows, cols), jnp.float32),
            pltpu.VMEM((fields, rows, cols), jnp.float32),
        ],
    )(slot_row, coupling, loading, stiffness, side)


def girth_side(blocks, axis, width, lanes):
    count = lax.axis_size(axis)
    forward = [(i, i + 1) for i in range(count - 1)]
    backward = [(target, source) for source, target in forward]
    lead = sum(block.shape[0] for block in blocks)
    rows = blocks[0].shape[1]
    size = blocks[0].shape[2]

    def pack(start):
        strip = jnp.concatenate([block[:, :, start : start + width] for block in blocks], axis=0)
        return jnp.swapaxes(strip, 1, 2).reshape(lead * width, rows)

    def unpack(flat):
        return jnp.swapaxes(flat.reshape(lead, width, rows), 1, 2)

    before = unpack(lax.ppermute(pack(size - width), axis, forward))
    after = unpack(lax.ppermute(pack(0), axis, backward))
    gap = jnp.zeros((lead, rows, lanes - 2 * width), before.dtype)
    return jnp.concatenate([after, gap, before], axis=2)


def chebyshev_weight(sweep):
    return 1.0 / (1.0 + 0.9 * math.cos(math.pi * (2 * sweep + 1) / (2 * SWEEPS)))


def operate_padded(padded, stiffness, coupling):
    centre = padded[:, 1:-1, 1:-1]
    beside = padded[:, 2:, 1:-1] + padded[:, :-2, 1:-1] + padded[:, 1:-1, 2:] + padded[:, 1:-1, :-2]
    mixing = jnp.einsum("ab,bij->aij", coupling, centre, precision=lax.Precision.HIGHEST)
    return stiffness * (4.0 * centre - beside) + mixing


def square_pairs(values, axis_at):
    first = jnp.take(values, 0, axis=axis_at)
    second = jnp.take(values, 1, axis=axis_at)
    third = jnp.take(values, 2, axis=axis_at)
    fourth = jnp.take(values, 3, axis=axis_at)
    return jnp.stack(
        [first * first + second * second, third * third + fourth * fourth], axis=axis_at
    )


def on_device(
    wave_amplitude,
    load_bank,
    freq_owner,
    thickness_class,
    class_stiffness,
    coupling,
    stress_map,
    psd_weight,
    hotspot_tile,
    hotspot_owner,
    prior_moments,
):
    row_count = wave_amplitude.shape[1]
    girth_cells = load_bank.shape[1]
    mode_count = load_bank.shape[0]
    width = SWEEPS - 1
    root = freq_owner[0]
    stiffness = jnp.zeros((row_count, girth_cells), jnp.float32)
    for level in range(class_stiffness.shape[0]):
        stiffness = stiffness + jnp.where(thickness_class == level, class_stiffness[level], 0.0)
    amplitude_ext = padded_2(wave_amplitude, (("length", 1),), width)
    stiffness_rows = padded_2(stiffness, (("length", 0),), width)
    factors = spread(load_bank, "girth", root, "length")
    ext_rows = row_count + 2 * width
    loading = jnp.dot(amplitude_ext.reshape(6 * ext_rows, mode_count), factors, preferred_element_type=jnp.float32)
    loading = loading.reshape(6, ext_rows, girth_cells)
    girth_count = lax.axis_size("girth")
    tile_ids = hotspot_tile[0]
    owner_ids = hotspot_owner[0, :, 0]
    listed = owner_ids.shape[0]
    positions = jnp.arange(listed, dtype=jnp.int32)
    matching = owner_ids[:, None] == owner_ids[None, :]
    earlier = positions[None, :] < positions[:, None]
    slot_rank = jnp.sum(jnp.logical_and(matching, earlier).astype(jnp.int32), axis=1)
    target = owner_ids * CAP + slot_rank
    slots = jnp.arange(girth_count * CAP, dtype=jnp.int32)
    hit = target[None, :] == slots[:, None]
    filled = jnp.any(hit, axis=1)
    slot_row = jnp.sum(jnp.where(hit, tile_ids[None, :], 0), axis=1)
    stiffness_at = jnp.take(stiffness, slot_row, axis=0)
    side = girth_side([loading, stiffness_rows[None]], "girth", width, 128)
    motion, motion_at = run_sweeps(slot_row, coupling, loading, stiffness_rows, side, row_count)
    stress_rows = stiffness_at[:, None, :] * jnp.einsum(
        "ka,aij->ikj", stress_map, motion_at, precision=lax.Precision.HIGHEST
    )
    spectra = square_pairs(stress_rows, 1)
    outbox = jnp.where(filled[:, None, None], spectra, 0.0)
    outbox = outbox.reshape(girth_count, CAP * 2 * girth_cells // 128, 128)
    received = lax.all_to_all(outbox, "girth", split_axis=0, concat_axis=0, tiled=True)
    received = received.reshape(girth_count, CAP, 2, girth_cells)
    hotspot_moments = prior_moments + (psd_weight[0] * received)[None, None]
    return (motion, hotspot_moments)


def solution(mesh):
    return jax.shard_map(
        on_device,
        mesh=mesh,
        in_specs=(
            P(None, "length", "girth"),
            P("girth", None),
            P(),
            P("length", "girth"),
            P(),
            P(),
            P(),
            P(),
            P("length", "girth"),
            P("length", "girth", None),
            P("length", "girth", None, None, None, None),
        ),
        out_specs=(P(None, "length", "girth"), P("length", "girth", None, None, None, None)),
        check_vma=False,
    )
```
